256 devices in a mesh: pair: 2 (over core), tr: 32 (over y, z), ch: 4 (over x).
Axes of the slice: x: 4, y: 4, z: 8, core: 2. Of those that a mesh axis runs over, the one named last changes fastest.
Arguments:
- post_gate: bfloat16 [32768, 512], P(('pair', 'tr'), 'ch'), may hold values from -6 to 6
- pre_gate: bfloat16 [32768, 512], P(('pair', 'tr'), 'ch'), may hold values from -6 to 6
- features: bfloat16 [32768, 512], P(('pair', 'tr'), 'ch'), may hold values from -6 to 6
- residues: float32 [512, 16], P('ch'), may hold values from -1.5 to 1.5
- rates: float32 [512, 16], P('ch'), may hold values from 1.5258789e-05 to 0.05
- skip: float32 [512], P('ch'), may hold values from -4 to 4
- out_weight: bfloat16 [512, 8192], P('ch'), may hold values from -0.375 to 0.375
Outputs:
- mixed: bfloat16 [32768, 8192], P(('pair', 'tr'), 'ch')
The draws below stay inside these ranges and needn't reach their ends.
All inputs are finite; a program needn't handle non-finite values.
Results may differ from the reference program's by a relative error of at most 0.0049.
Values may be sent and summed in bfloat16 or wider, within the bound.
No kernel may reach another device: no remote copies, remote signals or barrier semaphores. Data moves between devices by JAX's collectives and lax.ppermute only.
A program may use at most 128 MiB of HBM per device.

```python
import math
import jax
import jax.numpy as jnp
from jax import lax

DM = 8192
CH = 512
MODES = 16
TOK_DEV = 512
TOKENS = 32768


def raised(array, key, source, target, shards_of, factor):
    owner, partner = [(jnp.arange(array.shape[dim]) // (array.shape[dim] // shards_of)).reshape([-1 if axis == dim else 1 for axis in range(array.ndim)]) for dim in (source, target)]
    chosen = jax.random.permutation(key, shards_of)[partner]
    strong = (owner == chosen) | (owner == (partner + shards_of // 2) % shards_of)
    return jnp.where(strong, factor * array, array)


def block_scale(stream_key, extent, shards, low, high):
    factor_of, own = 1.0, jax.random.fold_in(stream_key, 6)
    for position, blocks in shards:
        draws = jnp.exp(jax.random.uniform(jax.random.fold_in(own, position), (blocks,), jnp.float32, low / len(shards), high / len(shards)))
        factor_of = factor_of * jnp.repeat(draws, extent[position] // blocks).reshape([-1 if axis == position else 1 for axis in range(len(extent))])
    return factor_of


def centred(own_key, extent, spread, reach, cuts=(), dtype=jnp.bfloat16):
    drawn = jax.random.normal(own_key, extent, jnp.float32) * spread
    if len(cuts) > 0:
        drawn = block_scale(own_key, extent, cuts, -0.22, 0.18) * drawn
    return jnp.clip(drawn, min=-reach, max=reach).astype(dtype)


def noise_with(own_key, extent, scale, bound, shards, heavy, kind=jnp.bfloat16):
    array = scale * jax.random.normal(own_key, extent, jnp.float32)
    if shards:
        array = array * block_scale(own_key, extent, shards, -0.22, 0.18)
    return jnp.clip(raised(array, jax.random.fold_in(own_key, 3), *heavy), -bound, bound).astype(kind)


def setup_inputs(seed: int = 0) -> dict:
    splits = jax.random.split(jax.random.key(seed), 8)
    post_gate = centred(splits[0], (TOKENS, CH), 1.0, 6.0, ((0, 64), (1, 4)))
    pre_gate = centred(splits[1], (TOKENS, CH), 1.0, 6.0, ((0, 64), (1, 4)))
    features = centred(splits[2], (TOKENS, CH), 1.0, 6.0, ((0, 64), (1, 4)))
    residues = centred(splits[3], (CH, MODES), 0.25, 1.5, ((0, 4),), jnp.float32)
    rates = jnp.clip(jnp.exp(math.log(0.05) - 8.094623 * jax.random.uniform(splits[4], (CH, MODES), jnp.float32) ** block_scale(splits[4], (CH, MODES), ((0, 4),), -0.2, 0.2)), 1.52587890625e-05, 0.05)
    skip = centred(splits[5], (CH,), 1.0, 4.0, ((0, 4),), jnp.float32)
    out_weight = noise_with(splits[6], (CH, DM), CH ** -0.5, 0.375, ((0, 4),), (0, 1, 4, 2.0))
    return dict(post_gate=post_gate, pre_gate=pre_gate, features=features, residues=residues, rates=rates, skip=skip, out_weight=out_weight)


def reference(post_gate, pre_gate, features, residues, rates, skip, out_weight):
    length = post_gate.shape[0]
    drive_term = pre_gate.astype(jnp.float32) * features.astype(jnp.float32)
    positions = jnp.arange(length).astype(jnp.float32)
    amplitude = residues * jnp.sqrt(-jnp.expm1(-2.0 * rates))

    def add_mode(running, mode_index):
        decay_rate = rates[:, mode_index]
        weight_now = amplitude[:, mode_index]
        return (running + weight_now[None, :] * jnp.exp(-decay_rate[None, :] * positions[:, None]), None)
    impulse, _ = lax.scan(add_mode, jnp.zeros(drive_term.shape, jnp.float32), jnp.arange(MODES))
    fft_len = 2 * length
    spectrum = jnp.fft.rfft(drive_term, n=fft_len, axis=0) * jnp.fft.rfft(impulse, n=fft_len, axis=0)
    convolved = jnp.fft.irfft(spectrum, n=fft_len, axis=0)[:length].astype(jnp.float32)
    gated_out = (post_gate.astype(jnp.float32) * (convolved + skip[None, :] * drive_term)).astype(jnp.bfloat16)
    row_blocks = gated_out.reshape(length // TOK_DEV, TOK_DEV, CH)

    def project(block_rows):
        return jnp.dot(block_rows, out_weight, preferred_element_type=jnp.float32).astype(jnp.bfloat16)
    return lax.map(project, row_blocks).reshape(length, DM)
```

```python
import jax
import jax.numpy as jnp
from jax import lax
from jax.sharding import PartitionSpec as P

CHUNK = 128


def sequence_place():
    return lax.axis_index("pair") * lax.axis_size("tr") + lax.axis_index("tr")


def split3(values):
    first = values.astype(jnp.bfloat16)
    rest = values - first.astype(jnp.float32)
    second = rest.astype(jnp.bfloat16)
    third = (rest - second.astype(jnp.float32)).astype(jnp.bfloat16)
    return first, second, third


def recurrent_convolve(drive_term, residues, rates):
    local_rows, local_chan = drive_term.shape
    modes = rates.shape[1]
    chunks = local_rows // CHUNK
    seq_devices = lax.axis_size("pair") * lax.axis_size("tr")
    seq_place = sequence_place()

    rate_nc = rates.T
    amplitude_nc = (residues * jnp.sqrt(-jnp.expm1(-2.0 * rates))).T
    step = jnp.arange(CHUNK, dtype=jnp.float32)[:, None, None]
    grow = jnp.exp(rate_nc[None] * step)
    rev = jnp.exp(-rate_nc[None] * (CHUNK - 1 - step))
    decay = amplitude_nc[None] * jnp.exp(-rate_nc[None] * step)

    x = drive_term.reshape(chunks, CHUNK, 1, local_chan)
    ends = jnp.sum(x * rev[None], axis=1)
    chunk_decay = jnp.exp(-rate_nc * CHUNK)
    local_states = []
    state = jnp.zeros_like(ends[0])
    for k in range(chunks):
        state = chunk_decay * state + ends[k]
        local_states.append(state)
    device_end = local_states[-1]

    gathered = lax.all_gather(device_end, ("pair", "tr"), axis=0, tiled=False)
    lag = (seq_place - 1 - jnp.arange(seq_devices, dtype=jnp.int32)).astype(jnp.float32)
    weight = jnp.where(
        lag[:, None, None] >= 0.0,
        jnp.exp(-rate_nc[None] * (local_rows * jnp.maximum(lag, 0.0))[:, None, None]),
        0.0,
    )
    history = jnp.sum(weight * gathered, axis=0)

    scaled = (x * grow[None]).reshape(chunks, CHUNK, modes * local_chan)
    parts = split3(scaled)
    lower = (step[:, 0, 0][:, None] >= step[:, 0, 0][None, :]).astype(jnp.bfloat16)
    lower3 = jnp.concatenate([lower, lower, lower], axis=1)
    stacked = jnp.concatenate(parts, axis=1)
    cums = jnp.einsum("ji,kiz->kjz", lower3, stacked, preferred_element_type=jnp.float32)
    cums = cums.reshape(chunks, CHUNK, modes, local_chan)

    one_step = jnp.exp(-rate_nc)
    entering = [history]
    for k in range(1, chunks):
        entering.append(local_states[k - 1] + jnp.exp(-rate_nc * (CHUNK * k)) * history)
    entering = jnp.stack(entering) * one_step[None]
    convolved = jnp.sum(decay[None] * (cums + entering[:, None]), axis=2)
    return convolved.reshape(local_rows, local_chan)


def local(post_gate, pre_gate, features, residues, rates, skip, out_weight):
    drive_term = pre_gate.astype(jnp.float32) * features.astype(jnp.float32)
    convolved = recurrent_convolve(drive_term, residues, rates)
    gated_out = (post_gate.astype(jnp.float32) * (convolved + skip[None, :] * drive_term)).astype(
        jnp.bfloat16
    )
    weight_cols = lax.all_to_all(out_weight, "ch", split_axis=1, concat_axis=0, tiled=True)
    mixed = jnp.dot(
        lax.all_gather(gated_out, "ch", axis=1, tiled=True),
        weight_cols,
        preferred_element_type=jnp.float32,
    )
    return mixed.astype(jnp.bfloat16)


def solution(mesh):
    in_specs = (
        P(("pair", "tr"), "ch"),
        P(("pair", "tr"), "ch"),
        P(("pair", "tr"), "ch"),
        P("ch", None),
        P("ch", None),
        P("ch"),
        P("ch", None),
    )
    out_specs = P(("pair", "tr"), "ch")
    return jax.shard_map(local, mesh=mesh, in_specs=in_specs, out_specs=out_specs, check_vma=False)
```

```python
import jax
import jax.numpy as jnp
from jax import lax
from jax.sharding import PartitionSpec as P

CHUNK = 128


def sequence_place():
    return lax.axis_index("pair") * lax.axis_size("tr") + lax.axis_index("tr")


def split3(values):
    first = lax.reduce_precision(values, exponent_bits=8, mantissa_bits=7)
    rest = values - first
    second = lax.reduce_precision(rest, exponent_bits=8, mantissa_bits=7)
    third = rest - second
    return (
        first.astype(jnp.bfloat16),
        second.astype(jnp.bfloat16),
        third.astype(jnp.bfloat16),
    )


def shift_seq(values, shift, seq_devices):
    pairs = [(src, src + shift) for src in range(seq_devices - shift)]
    return lax.ppermute(values, ("pair", "tr"), pairs)


def prefix_history(device_end, rate_nc, local_rows, seq_devices):
    radix = 8
    block_decay = -rate_nc * local_rows
    near = jnp.zeros_like(device_end)
    for m in range(1, radix + 1):
        near = near + jnp.exp(block_decay * (m - 1)) * shift_seq(device_end, m, seq_devices)
    history = near
    for q in range(1, seq_devices // radix):
        history = history + jnp.exp(block_decay * (radix * q)) * shift_seq(
            near, radix * q, seq_devices
        )
    return history


def recurrent_convolve(drive_term, residues, rates):
    local_rows, local_chan = drive_term.shape
    modes = rates.shape[1]
    chunks = local_rows // CHUNK
    seq_devices = lax.axis_size("pair") * lax.axis_size("tr")
    seq_place = sequence_place()

    rate_nc = rates.T
    amplitude_nc = (residues * jnp.sqrt(-jnp.expm1(-2.0 * rates))).T
    step = jnp.arange(CHUNK, dtype=jnp.float32)[:, None, None]
    grow = jnp.exp(rate_nc[None] * step)
    rev = jnp.exp(-rate_nc[None] * (CHUNK - 1 - step))
    decay = amplitude_nc[None] * jnp.exp(-rate_nc[None] * step)

    x = drive_term.reshape(chunks, CHUNK, 1, local_chan)
    ends = jnp.sum(x * rev[None], axis=1)
    chunk_decay = jnp.exp(-rate_nc * CHUNK)
    local_states = []
    state = jnp.zeros_like(ends[0])
    for k in range(chunks):
        state = chunk_decay * state + ends[k]
        local_states.append(state)
    device_end = local_states[-1]

    history = prefix_history(device_end, rate_nc, local_rows, seq_devices)

    scaled = (x * grow[None]).reshape(chunks, CHUNK, modes * local_chan)
    parts = split3(scaled)
    lower = (step[:, 0, 0][:, None] >= step[:, 0, 0][None, :]).astype(jnp.bfloat16)
    lower3 = jnp.concatenate([lower, lower, lower], axis=1)
    stacked = jnp.concatenate(parts, axis=1)
    cums = jnp.einsum("ji,kiz->kjz", lower3, stacked, preferred_element_type=jnp.float32)
    cums = cums.reshape(chunks, CHUNK, modes, local_chan)

    one_step = jnp.exp(-rate_nc)
    entering = [history]
    for k in range(1, chunks):
        entering.append(local_states[k - 1] + jnp.exp(-rate_nc * (CHUNK * k)) * history)
    entering = jnp.stack(entering) * one_step[None]
    convolved = jnp.sum(decay[None] * (cums + entering[:, None]), axis=2)
    return convolved.reshape(local_rows, local_chan)


def local(post_gate, pre_gate, features, residues, rates, skip, out_weight):
    drive_term = pre_gate.astype(jnp.float32) * features.astype(jnp.float32)
    convolved = recurrent_convolve(drive_term, residues, rates)
    gated_out = (post_gate.astype(jnp.float32) * (convolved + skip[None, :] * drive_term)).astype(
        jnp.bfloat16
    )
    ch_size = lax.axis_size("ch")
    ch_place = lax.axis_index("ch")
    cols = out_weight.shape[1] // ch_size

    def weight_for(offset):
        start = ((ch_place + offset) % ch_size) * cols
        return lax.dynamic_slice_in_dim(out_weight, start, cols, axis=1)

    mixed = jnp.dot(gated_out, weight_for(0), preferred_element_type=jnp.float32)
    for k in range(1, ch_size):
        ring = [(src, (src + k) % ch_size) for src in range(ch_size)]
        rows_k = lax.ppermute(weight_for(k), "ch", ring)
        gated_k = lax.ppermute(gated_out, "ch", ring)
        mixed = mixed + jnp.dot(gated_k, rows_k, preferred_element_type=jnp.float32)
    return mixed.astype(jnp.bfloat16)


def solution(mesh):
    in_specs = (
        P(("pair", "tr"), "ch"),
        P(("pair", "tr"), "ch"),
        P(("pair", "tr"), "ch"),
        P("ch", None),
        P("ch", None),
        P("ch"),
        P("ch", None),
    )
    out_specs = P(("pair", "tr"), "ch")
    return jax.shard_map(local, mesh=mesh, in_specs=in_specs, out_specs=out_specs, check_vma=False)
```

```python
import jax
import jax.numpy as jnp
from jax import lax
from jax.sharding import PartitionSpec as P

CHUNK = 128


def sequence_place():
    return lax.axis_index("pair") * lax.axis_size("tr") + lax.axis_index("tr")


def split3(values):
    first = lax.reduce_precision(values, exponent_bits=8, mantissa_bits=7)
    rest = values - first
    second = lax.reduce_precision(rest, exponent_bits=8, mantissa_bits=7)
    third = rest - second
    return (
        first.astype(jnp.bfloat16),
        second.astype(jnp.bfloat16),
        third.astype(jnp.bfloat16),
    )


def prefix_history(device_end, rate_nc, local_rows, seq_devices, seq_place):
    lag = (jnp.arange(seq_devices, dtype=jnp.int32) - 1 - seq_place).astype(jnp.float32)
    weight = jnp.where(
        lag[:, None, None] >= 0.0,
        jnp.exp(-rate_nc[None] * (local_rows * jnp.maximum(lag, 0.0))[:, None, None]),
        0.0,
    )
    sent = lax.all_to_all(weight * device_end[None], ("pair", "tr"), 0, 0, tiled=True)
    return jnp.sum(sent, axis=0)


def recurrent_convolve(drive_term, residues, rates):
    local_rows, local_chan = drive_term.shape
    modes = rates.shape[1]
    chunks = local_rows // CHUNK
    seq_devices = lax.axis_size("pair") * lax.axis_size("tr")
    seq_place = sequence_place()

    rate_nc = rates.T
    amplitude_nc = (residues * jnp.sqrt(-jnp.expm1(-2.0 * rates))).T
    step = jnp.arange(CHUNK, dtype=jnp.float32)[:, None, None]
    grow = jnp.exp(rate_nc[None] * step)
    rev = jnp.exp(-rate_nc[None] * (CHUNK - 1 - step))
    decay = amplitude_nc[None] * jnp.exp(-rate_nc[None] * step)

    x = drive_term.reshape(chunks, CHUNK, 1, local_chan)
    ends = jnp.sum(x * rev[None], axis=1)
    chunk_decay = jnp.exp(-rate_nc * CHUNK)
    local_states = []
    state = jnp.zeros_like(ends[0])
    for k in range(chunks):
        state = chunk_decay * state + ends[k]
        local_states.append(state)
    device_end = local_states[-1]

    history = prefix_history(device_end, rate_nc, local_rows, seq_devices, seq_place)

    scaled = (x * grow[None]).reshape(chunks, CHUNK, modes * local_chan)
    parts = split3(scaled)
    lower = (step[:, 0, 0][:, None] >= step[:, 0, 0][None, :]).astype(jnp.bfloat16)
    lower3 = jnp.concatenate([lower, lower, lower], axis=1)
    stacked = jnp.concatenate(parts, axis=1)
    cums = jnp.einsum("ji,kiz->kjz", lower3, stacked, preferred_element_type=jnp.float32)
    cums = cums.reshape(chunks, CHUNK, modes, local_chan)

    one_step = jnp.exp(-rate_nc)
    entering = [history]
    for k in range(1, chunks):
        entering.append(local_states[k - 1] + jnp.exp(-rate_nc * (CHUNK * k)) * history)
    entering = jnp.stack(entering) * one_step[None]
    convolved = jnp.sum(decay[None] * (cums + entering[:, None]), axis=2)
    return convolved.reshape(local_rows, local_chan)


def local(post_gate, pre_gate, features, residues, rates, skip, out_weight):
    drive_term = pre_gate.astype(jnp.float32) * features.astype(jnp.float32)
    convolved = recurrent_convolve(drive_term, residues, rates)
    gated_out = (post_gate.astype(jnp.float32) * (convolved + skip[None, :] * drive_term)).astype(
        jnp.bfloat16
    )
    ch_size = lax.axis_size("ch")
    ch_place = lax.axis_index("ch")
    cols = out_weight.shape[1] // ch_size

    def weight_for(offset):
        start = ((ch_place + offset) % ch_size) * cols
        return lax.dynamic_slice_in_dim(out_weight, start, cols, axis=1)

    mixed = jnp.dot(gated_out, weight_for(0), preferred_element_type=jnp.float32)
    for k in range(1, ch_size):
        ring = [(src, (src + k) % ch_size) for src in range(ch_size)]
        rows_k = lax.ppermute(weight_for(k), "ch", ring)
        gated_k = lax.ppermute(gated_out, "ch", ring)
        mixed = mixed + jnp.dot(gated_k, rows_k, preferred_element_type=jnp.float32)
    return mixed.astype(jnp.bfloat16)


def solution(mesh):
    in_specs = (
        P(("pair", "tr"), "ch"),
        P(("pair", "tr"), "ch"),
        P(("pair", "tr"), "ch"),
        P("ch", None),
        P("ch", None),
        P("ch"),
        P("ch", None),
    )
    out_specs = P(("pair", "tr"), "ch")
    return jax.shard_map(local, mesh=mesh, in_specs=in_specs, out_specs=out_specs, check_vma=False)
```

```python
import jax
import jax.numpy as jnp
from jax import lax
from jax.sharding import PartitionSpec as P

CHUNK = 128


def sequence_place():
    return lax.axis_index("pair") * lax.axis_size("tr") + lax.axis_index("tr")


def split3(values):
    first = lax.reduce_precision(values, exponent_bits=8, mantissa_bits=7)
    rest = values - first
    second = lax.reduce_precision(rest, exponent_bits=8, mantissa_bits=7)
    third = rest - second
    return (
        first.astype(jnp.bfloat16),
        second.astype(jnp.bfloat16),
        third.astype(jnp.bfloat16),
    )


def prefix_history(device_end, rate_nc, local_rows, seq_devices, seq_place, out_weight):
    lag = (jnp.arange(seq_devices, dtype=jnp.int32) - 1 - seq_place).astype(jnp.float32)
    weight = jnp.where(
        lag[:, None, None] >= 0.0,
        jnp.exp(-rate_nc[None] * (local_rows * jnp.maximum(lag, 0.0))[:, None, None]),
        0.0,
    )
    payload, out_weight = lax.optimization_barrier((weight * device_end[None], out_weight))
    sent = lax.all_to_all(payload, ("pair", "tr"), 0, 0, tiled=True)
    return jnp.sum(sent, axis=0), out_weight


def recurrent_convolve(drive_term, residues, rates, out_weight):
    local_rows, local_chan = drive_term.shape
    modes = rates.shape[1]
    chunks = local_rows // CHUNK
    seq_devices = lax.axis_size("pair") * lax.axis_size("tr")
    seq_place = sequence_place()

    rate_nc = rates.T
    amplitude_nc = (residues * jnp.sqrt(-jnp.expm1(-2.0 * rates))).T
    step = jnp.arange(CHUNK, dtype=jnp.float32)[:, None, None]
    grow = jnp.exp(rate_nc[None] * step)
    rev = jnp.exp(-rate_nc[None] * (CHUNK - 1 - step))
    decay = amplitude_nc[None] * jnp.exp(-rate_nc[None] * step)

    x = drive_term.reshape(chunks, CHUNK, 1, local_chan)
    ends = jnp.sum(x * rev[None], axis=1)
    chunk_decay = jnp.exp(-rate_nc * CHUNK)
    local_states = []
    state = jnp.zeros_like(ends[0])
    for k in range(chunks):
        state = chunk_decay * state + ends[k]
        local_states.append(state)
    device_end = local_states[-1]

    history, out_weight = prefix_history(device_end, rate_nc, local_rows, seq_devices, seq_place, out_weight)

    scaled = (x * grow[None]).reshape(chunks, CHUNK, modes * local_chan)
    parts = split3(scaled)
    lower = (step[:, 0, 0][:, None] >= step[:, 0, 0][None, :]).astype(jnp.bfloat16)
    lower3 = jnp.concatenate([lower, lower, lower], axis=1)
    stacked = jnp.concatenate(parts, axis=1)
    cums = jnp.einsum("ji,kiz->kjz", lower3, stacked, preferred_element_type=jnp.float32)
    cums = cums.reshape(chunks, CHUNK, modes, local_chan)

    one_step = jnp.exp(-rate_nc)
    entering = [history]
    for k in range(1, chunks):
        entering.append(local_states[k - 1] + jnp.exp(-rate_nc * (CHUNK * k)) * history)
    entering = jnp.stack(entering) * one_step[None]
    convolved = jnp.sum(decay[None] * (cums + entering[:, None]), axis=2)
    return convolved.reshape(local_rows, local_chan), out_weight


def local(post_gate, pre_gate, features, residues, rates, skip, out_weight):
    drive_term = pre_gate.astype(jnp.float32) * features.astype(jnp.float32)
    convolved, out_weight = recurrent_convolve(drive_term, residues, rates, out_weight)
    gated_out = (post_gate.astype(jnp.float32) * (convolved + skip[None, :] * drive_term)).astype(
        jnp.bfloat16
    )
    ch_size = lax.axis_size("ch")
    ch_place = lax.axis_index("ch")
    cols = out_weight.shape[1] // ch_size

    def weight_for(offset):
        start = ((ch_place + offset) % ch_size) * cols
        return lax.dynamic_slice_in_dim(out_weight, start, cols, axis=1)

    gated_parts = [gated_out]
    weight_parts = [weight_for(0)]
    for k in range(1, ch_size):
        ring = [(src, (src + k) % ch_size) for src in range(ch_size)]
        weight_parts.append(lax.ppermute(weight_for(k), "ch", ring))
        gated_parts.append(lax.ppermute(gated_out, "ch", ring))
    mixed = jnp.dot(
        jnp.concatenate(gated_parts, axis=1),
        jnp.concatenate(weight_parts, axis=0),
        preferred_element_type=jnp.float32,
    )
    return mixed.astype(jnp.bfloat16)


def solution(mesh):
    in_specs = (
        P(("pair", "tr"), "ch"),
        P(("pair", "tr"), "ch"),
        P(("pair", "tr"), "ch"),
        P("ch", None),
        P("ch", None),
        P("ch"),
        P("ch", None),
    )
    out_specs = P(("pair", "tr"), "ch")
    return jax.shard_map(local, mesh=mesh, in_specs=in_specs, out_specs=out_specs, check_vma=False)
```

```python
import jax
import jax.numpy as jnp
from jax import lax
from jax.sharding import PartitionSpec as P

CHUNK = 128


def sequence_place():
    return lax.axis_index("pair") * lax.axis_size("tr") + lax.axis_index("tr")


def split3(values):
    first = lax.reduce_precision(values, exponent_bits=8, mantissa_bits=7)
    rest = values - first
    second = lax.reduce_precision(rest, exponent_bits=8, mantissa_bits=7)
    third = rest - second
    return (
        first.astype(jnp.bfloat16),
        second.astype(jnp.bfloat16),
        third.astype(jnp.bfloat16),
    )


def prefix_history(device_end, rate_nc, local_rows, seq_devices, seq_place, out_weight):
    lag = (jnp.arange(seq_devices, dtype=jnp.int32) - 1 - seq_place).astype(jnp.float32)
    weight = jnp.where(
        lag[:, None, None] >= 0.0,
        jnp.exp(-rate_nc[None] * (local_rows * jnp.maximum(lag, 0.0))[:, None, None]),
        0.0,
    )
    payload, out_weight = lax.optimization_barrier((weight * device_end[None], out_weight))
    sent = lax.all_to_all(payload, ("pair", "tr"), 0, 0, tiled=True)
    return jnp.sum(sent, axis=0), out_weight


def recurrent_convolve(drive_term, residues, rates, out_weight):
    local_rows, local_chan = drive_term.shape
    modes = rates.shape[1]
    chunks = local_rows // CHUNK
    seq_devices = lax.axis_size("pair") * lax.axis_size("tr")
    seq_place = sequence_place()

    rate_nc = rates.T
    amplitude_nc = (residues * jnp.sqrt(-jnp.expm1(-2.0 * rates))).T
    step = jnp.arange(CHUNK, dtype=jnp.float32)[:, None, None]
    grow = jnp.exp(rate_nc[None] * step)
    rev = jnp.exp(-rate_nc[None] * (CHUNK - 1 - step))
    decay = amplitude_nc[None] * jnp.exp(-rate_nc[None] * step)

    x = drive_term.reshape(chunks, CHUNK, 1, local_chan)
    ends = jnp.sum(x * rev[None], axis=1)
    chunk_decay = jnp.exp(-rate_nc * CHUNK)
    local_states = []
    state = jnp.zeros_like(ends[0])
    for k in range(chunks):
        state = chunk_decay * state + ends[k]
        local_states.append(state)
    device_end = local_states[-1]

    history, out_weight = prefix_history(device_end, rate_nc, local_rows, seq_devices, seq_place, out_weight)

    scaled = (x * grow[None]).reshape(chunks, CHUNK, modes * local_chan)
    parts = split3(scaled)
    lower = (step[:, 0, 0][:, None] >= step[:, 0, 0][None, :]).astype(jnp.bfloat16)
    lower3 = jnp.concatenate([lower, lower, lower], axis=1)
    stacked = jnp.concatenate(parts, axis=1)
    cums = jnp.einsum("ji,kiz->kjz", lower3, stacked, preferred_element_type=jnp.float32)
    cums = cums.reshape(chunks, CHUNK, modes, local_chan)

    one_step = jnp.exp(-rate_nc)
    entering = [history]
    for k in range(1, chunks):
        entering.append(local_states[k - 1] + jnp.exp(-rate_nc * (CHUNK * k)) * history)
    entering = jnp.stack(entering) * one_step[None]
    convolved = jnp.sum(decay[None] * (cums + entering[:, None]), axis=2)
    return convolved.reshape(local_rows, local_chan), out_weight


def local(post_gate, pre_gate, features, residues, rates, skip, out_weight):
    drive_term = pre_gate.astype(jnp.float32) * features.astype(jnp.float32)
    convolved, out_weight = recurrent_convolve(drive_term, residues, rates, out_weight)
    gated_out = (post_gate.astype(jnp.float32) * (convolved + skip[None, :] * drive_term)).astype(
        jnp.bfloat16
    )
    ch_size = lax.axis_size("ch")
    ch_place = lax.axis_index("ch")
    core = lax.axis_index("pair")
    cols = out_weight.shape[1] // ch_size
    half = cols // 2

    def weight_for(offset, width, part):
        start = ((ch_place + offset) % ch_size) * cols + part * width
        return lax.dynamic_slice_in_dim(out_weight, start, width, axis=1)

    pieces = []
    gated_parts = [gated_out]
    for k in range(1, ch_size):
        ring = [(src, (src + k) % ch_size) for src in range(ch_size)]
        pieces.append(lax.ppermute(weight_for(k, half, core), "ch", ring))
        gated_parts.append(lax.ppermute(gated_out, "ch", ring))
    fetched = jnp.stack(pieces)
    swapped = lax.ppermute(fetched, "pair", [(0, 1), (1, 0)])
    remote = jnp.zeros((ch_size - 1, fetched.shape[1], cols), out_weight.dtype)
    remote = lax.dynamic_update_slice_in_dim(remote, fetched, core * half, axis=2)
    remote = lax.dynamic_update_slice_in_dim(remote, swapped, (1 - core) * half, axis=2)
    weight_rows = jnp.concatenate(
        [weight_for(0, cols, 0), remote.reshape(-1, cols)], axis=0
    )
    mixed = jnp.dot(
        jnp.concatenate(gated_parts, axis=1),
        weight_rows,
        preferred_element_type=jnp.float32,
    )
    return mixed.astype(jnp.bfloat16)


def solution(mesh):
    in_specs = (
        P(("pair", "tr"), "ch"),
        P(("pair", "tr"), "ch"),
        P(("pair", "tr"), "ch"),
        P("ch", None),
        P("ch", None),
        P("ch"),
        P("ch", None),
    )
    out_specs = P(("pair", "tr"), "ch")
    return jax.shard_map(local, mesh=mesh, in_specs=in_specs, out_specs=out_specs, check_vma=False)
```

```python
import jax
import jax.numpy as jnp
from jax import lax
from jax.sharding import PartitionSpec as P

CHUNK = 128


def sequence_place():
    return lax.axis_index("pair") * lax.axis_size("tr") + lax.axis_index("tr")


def split3(values):
    first = lax.reduce_precision(values, exponent_bits=8, mantissa_bits=7)
    rest = values - first
    second = lax.reduce_precision(rest, exponent_bits=8, mantissa_bits=7)
    third = rest - second
    return (
        first.astype(jnp.bfloat16),
        second.astype(jnp.bfloat16),
        third.astype(jnp.bfloat16),
    )


def prefix_history(device_end, rate_nc, local_rows, seq_devices, seq_place):
    lag = (jnp.arange(seq_devices, dtype=jnp.int32) - 1 - seq_place).astype(jnp.float32)
    weight = jnp.where(
        lag[:, None, None] >= 0.0,
        jnp.exp(-rate_nc[None] * (local_rows * jnp.maximum(lag, 0.0))[:, None, None]),
        0.0,
    )
    return weight * device_end[None]


def recurrent_convolve(drive_term, residues, rates, out_weight):
    local_rows, local_chan = drive_term.shape
    modes = rates.shape[1]
    chunks = local_rows // CHUNK
    seq_devices = lax.axis_size("pair") * lax.axis_size("tr")
    seq_place = sequence_place()

    rate_nc = rates.T
    step = jnp.arange(CHUNK, dtype=jnp.float32)[:, None, None]
    rev = jnp.exp(-rate_nc[None] * (CHUNK - 1 - step))

    x = drive_term.reshape(chunks, CHUNK, 1, local_chan)
    ends = jnp.sum(x * rev[None], axis=1)
    chunk_decay = jnp.exp(-rate_nc * CHUNK)
    local_states = []
    state = jnp.zeros_like(ends[0])
    for k in range(chunks):
        state = chunk_decay * state + ends[k]
        local_states.append(state)
    payload = prefix_history(local_states[-1], rate_nc, local_rows, seq_devices, seq_place)
    payload, out_weight, x, rate_nc, residues = lax.optimization_barrier(
        (payload, out_weight, x, rate_nc, residues)
    )
    sent = lax.all_to_all(payload, ("pair", "tr"), 0, 0, tiled=True)

    amplitude_nc = (residues * jnp.sqrt(-jnp.expm1(-2.0 * rates))).T
    grow = jnp.exp(rate_nc[None] * step)
    decay = amplitude_nc[None] * jnp.exp(-rate_nc[None] * step)
    scaled = (x * grow[None]).reshape(chunks, CHUNK, modes * local_chan)
    parts = split3(scaled)
    lower = (step[:, 0, 0][:, None] >= step[:, 0, 0][None, :]).astype(jnp.bfloat16)
    lower3 = jnp.concatenate([lower, lower, lower], axis=1)
    stacked = jnp.concatenate(parts, axis=1)
    cums = jnp.einsum("ji,kiz->kjz", lower3, stacked, preferred_element_type=jnp.float32)
    cums = cums.reshape(chunks, CHUNK, modes, local_chan)
    within = jnp.sum(decay[None] * cums, axis=2)

    history = jnp.sum(sent, axis=0)
    one_step = jnp.exp(-rate_nc)
    entering = [history]
    for k in range(1, chunks):
        entering.append(local_states[k - 1] + jnp.exp(-rate_nc * (CHUNK * k)) * history)
    entering = jnp.stack(entering) * one_step[None]
    convolved = within + jnp.sum(decay[None] * entering[:, None], axis=2)
    return convolved.reshape(local_rows, local_chan), out_weight


def local(post_gate, pre_gate, features, residues, rates, skip, out_weight):
    drive_term = pre_gate.astype(jnp.float32) * features.astype(jnp.float32)
    convolved, out_weight = recurrent_convolve(drive_term, residues, rates, out_weight)
    gated_out = (post_gate.astype(jnp.float32) * (convolved + skip[None, :] * drive_term)).astype(
        jnp.bfloat16
    )
    ch_size = lax.axis_size("ch")
    ch_place = lax.axis_index("ch")
    core = lax.axis_index("pair")
    cols = out_weight.shape[1] // ch_size
    half = cols // 2

    def weight_for(offset, width, part):
        start = ((ch_place + offset) % ch_size) * cols + part * width
        return lax.dynamic_slice_in_dim(out_weight, start, width, axis=1)

    pieces = []
    gated_parts = [gated_out]
    for k in range(1, ch_size):
        ring = [(src, (src + k) % ch_size) for src in range(ch_size)]
        pieces.append(lax.ppermute(weight_for(k, half, core), "ch", ring))
        gated_parts.append(lax.ppermute(gated_out, "ch", ring))
    fetched = jnp.stack(pieces)
    swapped = lax.ppermute(fetched, "pair", [(0, 1), (1, 0)])
    remote = jnp.zeros((ch_size - 1, fetched.shape[1], cols), out_weight.dtype)
    remote = lax.dynamic_update_slice_in_dim(remote, fetched, core * half, axis=2)
    remote = lax.dynamic_update_slice_in_dim(remote, swapped, (1 - core) * half, axis=2)
    weight_rows = jnp.concatenate(
        [weight_for(0, cols, 0), remote.reshape(-1, cols)], axis=0
    )
    mixed = jnp.dot(
        jnp.concatenate(gated_parts, axis=1),
        weight_rows,
        preferred_element_type=jnp.float32,
    )
    return mixed.astype(jnp.bfloat16)


def solution(mesh):
    in_specs = (
        P(("pair", "tr"), "ch"),
        P(("pair", "tr"), "ch"),
        P(("pair", "tr"), "ch"),
        P("ch", None),
        P("ch", None),
        P("ch"),
        P("ch", None),
    )
    out_specs = P(("pair", "tr"), "ch")
    return jax.shard_map(local, mesh=mesh, in_specs=in_specs, out_specs=out_specs, check_vma=False)
```

```python
import jax
import jax.numpy as jnp
from jax import lax
from jax.sharding import PartitionSpec as P

CHUNK = 128


def sequence_place():
    return lax.axis_index("pair") * lax.axis_size("tr") + lax.axis_index("tr")


def split3(values):
    first = lax.reduce_precision(values, exponent_bits=8, mantissa_bits=7)
    rest = values - first
    second = lax.reduce_precision(rest, exponent_bits=8, mantissa_bits=7)
    third = rest - second
    return (
        first.astype(jnp.bfloat16),
        second.astype(jnp.bfloat16),
        third.astype(jnp.bfloat16),
    )


def prefix_history(device_end, rate_nc, local_rows, seq_devices, seq_place):
    lag = (jnp.arange(seq_devices, dtype=jnp.int32) - 1 - seq_place).astype(jnp.float32)
    weight = jnp.where(
        lag[:, None, None] >= 0.0,
        jnp.exp(-rate_nc[None] * (local_rows * jnp.maximum(lag, 0.0))[:, None, None]),
        0.0,
    )
    return weight * device_end[None]


def recurrent_convolve(drive_term, residues, rates, out_weight):
    local_rows, local_chan = drive_term.shape
    modes = rates.shape[1]
    chunks = local_rows // CHUNK
    seq_devices = lax.axis_size("pair") * lax.axis_size("tr")
    seq_place = sequence_place()

    rate_nc = rates.T
    step = jnp.arange(CHUNK, dtype=jnp.float32)[:, None, None]
    rev = jnp.exp(-rate_nc[None] * (CHUNK - 1 - step))

    x = drive_term.reshape(chunks, CHUNK, 1, local_chan)
    ends = jnp.sum(x * rev[None], axis=1)
    chunk_decay = jnp.exp(-rate_nc * CHUNK)
    local_states = []
    state = jnp.zeros_like(ends[0])
    for k in range(chunks):
        state = chunk_decay * state + ends[k]
        local_states.append(state)
    payload = prefix_history(local_states[-1], rate_nc, local_rows, seq_devices, seq_place)
    payload, out_weight, x, rate_nc, residues = lax.optimization_barrier(
        (payload, out_weight, x, rate_nc, residues)
    )
    sent = lax.all_to_all(payload, ("pair", "tr"), 0, 0, tiled=True)

    amplitude_nc = (residues * jnp.sqrt(-jnp.expm1(-2.0 * rates))).T
    grow = jnp.exp(rate_nc[None] * step)
    decay = amplitude_nc[None] * jnp.exp(-rate_nc[None] * step)
    scaled = (x * grow[None]).reshape(chunks, CHUNK, modes * local_chan)
    parts = split3(scaled)
    lower = (step[:, 0, 0][:, None] >= step[:, 0, 0][None, :]).astype(jnp.bfloat16)
    lower3 = jnp.concatenate([lower, lower, lower], axis=1)
    stacked = jnp.concatenate(parts, axis=1)
    cums = jnp.einsum("ji,kiz->kjz", lower3, stacked, preferred_element_type=jnp.float32)
    cums = cums.reshape(chunks, CHUNK, modes, local_chan)
    within = jnp.sum(decay[None] * cums, axis=2)

    within, sent = lax.optimization_barrier((within, sent))
    history = jnp.sum(sent, axis=0)
    one_step = jnp.exp(-rate_nc)
    entering = [history]
    for k in range(1, chunks):
        entering.append(local_states[k - 1] + jnp.exp(-rate_nc * (CHUNK * k)) * history)
    entering = jnp.stack(entering) * one_step[None]
    convolved = within + jnp.sum(decay[None] * entering[:, None], axis=2)
    return convolved.reshape(local_rows, local_chan), out_weight


def local(post_gate, pre_gate, features, residues, rates, skip, out_weight):
    drive_term = pre_gate.astype(jnp.float32) * features.astype(jnp.float32)
    convolved, out_weight = recurrent_convolve(drive_term, residues, rates, out_weight)
    gated_out = (post_gate.astype(jnp.float32) * (convolved + skip[None, :] * drive_term)).astype(
        jnp.bfloat16
    )
    ch_size = lax.axis_size("ch")
    ch_place = lax.axis_index("ch")
    core = lax.axis_index("pair")
    cols = out_weight.shape[1] // ch_size
    half = cols // 2

    def weight_for(offset, width, part):
        start = ((ch_place + offset) % ch_size) * cols + part * width
        return lax.dynamic_slice_in_dim(out_weight, start, width, axis=1)

    pieces = []
    gated_parts = [gated_out]
    for k in range(1, ch_size):
        ring = [(src, (src + k) % ch_size) for src in range(ch_size)]
        pieces.append(lax.ppermute(weight_for(k, half, core), "ch", ring))
        gated_parts.append(lax.ppermute(gated_out, "ch", ring))
    fetched = jnp.stack(pieces)
    swapped = lax.ppermute(fetched, "pair", [(0, 1), (1, 0)])
    remote = jnp.zeros((ch_size - 1, fetched.shape[1], cols), out_weight.dtype)
    remote = lax.dynamic_update_slice_in_dim(remote, fetched, core * half, axis=2)
    remote = lax.dynamic_update_slice_in_dim(remote, swapped, (1 - core) * half, axis=2)
    weight_rows = jnp.concatenate(
        [weight_for(0, cols, 0), remote.reshape(-1, cols)], axis=0
    )
    mixed = jnp.dot(
        jnp.concatenate(gated_parts, axis=1),
        weight_rows,
        preferred_element_type=jnp.float32,
    )
    return mixed.astype(jnp.bfloat16)


def solution(mesh):
    in_specs = (
        P(("pair", "tr"), "ch"),
        P(("pair", "tr"), "ch"),
        P(("pair", "tr"), "ch"),
        P("ch", None),
        P("ch", None),
        P("ch"),
        P("ch", None),
    )
    out_specs = P(("pair", "tr"), "ch")
    return jax.shard_map(local, mesh=mesh, in_specs=in_specs, out_specs=out_specs, check_vma=False)
```

```python
import jax
import jax.numpy as jnp
from jax import lax
from jax.sharding import PartitionSpec as P

CHUNK = 128


def sequence_place():
    return lax.axis_index("pair") * lax.axis_size("tr") + lax.axis_index("tr")


def split3(values):
    first = lax.reduce_precision(values, exponent_bits=8, mantissa_bits=7)
    rest = values - first
    second = lax.reduce_precision(rest, exponent_bits=8, mantissa_bits=7)
    third = rest - second
    return (
        first.astype(jnp.bfloat16),
        second.astype(jnp.bfloat16),
        third.astype(jnp.bfloat16),
    )


def prefix_history(device_end, rate_nc, local_rows, seq_devices, seq_place):
    lag = (jnp.arange(seq_devices, dtype=jnp.int32) - 1 - seq_place).astype(jnp.float32)
    weight = jnp.where(
        lag[:, None, None] >= 0.0,
        jnp.exp(-rate_nc[None] * (local_rows * jnp.maximum(lag, 0.0))[:, None, None]),
        0.0,
    )
    return weight * device_end[None]


def recurrent_convolve(drive_term, residues, rates, out_weight):
    local_rows, local_chan = drive_term.shape
    modes = rates.shape[1]
    chunks = local_rows // CHUNK
    seq_devices = lax.axis_size("pair") * lax.axis_size("tr")
    seq_place = sequence_place()

    rate_nc = rates.T
    step = jnp.arange(CHUNK, dtype=jnp.float32)[:, None, None]
    rev = jnp.exp(-rate_nc[None] * (CHUNK - 1 - step))

    x = drive_term.reshape(chunks, CHUNK, 1, local_chan)
    ends = jnp.sum(x * rev[None], axis=1)
    chunk_decay = jnp.exp(-rate_nc * CHUNK)
    local_states = []
    state = jnp.zeros_like(ends[0])
    for k in range(chunks):
        state = chunk_decay * state + ends[k]
        local_states.append(state)
    payload = prefix_history(local_states[-1], rate_nc, local_rows, seq_devices, seq_place)
    payload, out_weight, x, rate_nc, residues = lax.optimization_barrier(
        (payload, out_weight, x, rate_nc, residues)
    )
    sent = lax.all_to_all(payload, ("pair", "tr"), 0, 0, tiled=True)

    amplitude_nc = (residues * jnp.sqrt(-jnp.expm1(-2.0 * rates))).T
    grow = jnp.exp(rate_nc[None] * step)
    decay = amplitude_nc[None] * jnp.exp(-rate_nc[None] * step)
    scaled = (x * grow[None]).reshape(chunks, CHUNK, modes * local_chan)
    parts = split3(scaled)
    lower = (step[:, 0, 0][:, None] >= step[:, 0, 0][None, :]).astype(jnp.bfloat16)
    lower3 = jnp.concatenate([lower, lower, lower], axis=1)
    stacked = jnp.concatenate(parts, axis=1)
    cums = jnp.einsum("ji,kiz->kjz", lower3, stacked, preferred_element_type=jnp.float32)
    cums = cums.reshape(chunks, CHUNK, modes, local_chan)
    within = jnp.sum(decay[None] * cums, axis=2)

    within, sent = lax.optimization_barrier((within, sent))
    history = jnp.sum(sent, axis=0)
    one_step = jnp.exp(-rate_nc)
    entering = [history]
    for k in range(1, chunks):
        entering.append(local_states[k - 1] + jnp.exp(-rate_nc * (CHUNK * k)) * history)
    entering = jnp.stack(entering) * one_step[None]
    convolved = within + jnp.sum(decay[None] * entering[:, None], axis=2)
    return convolved.reshape(local_rows, local_chan), out_weight


def local(post_gate, pre_gate, features, residues, rates, skip, out_weight):
    drive_term = pre_gate.astype(jnp.float32) * features.astype(jnp.float32)
    convolved, out_weight = recurrent_convolve(drive_term, residues, rates, out_weight)
    gated_out = (post_gate.astype(jnp.float32) * (convolved + skip[None, :] * drive_term)).astype(
        jnp.bfloat16
    )
    ch_size = lax.axis_size("ch")
    ch_place = lax.axis_index("ch")
    core = lax.axis_index("pair")
    cols = out_weight.shape[1] // ch_size
    half = cols // 2

    def weight_for(offset, width, part):
        start = ((ch_place + offset) % ch_size) * cols + part * width
        return lax.dynamic_slice_in_dim(out_weight, start, width, axis=1)

    pieces = []
    for k in range(1, ch_size):
        ring = [(src, (src + k) % ch_size) for src in range(ch_size)]
        pieces.append(lax.ppermute(weight_for(k, half, core), "ch", ring))
    fetched = jnp.stack(pieces)
    swapped = lax.ppermute(fetched, "pair", [(0, 1), (1, 0)])
    gated_out, fetched = lax.optimization_barrier((gated_out, fetched))
    gated_parts = [gated_out]
    for k in range(1, ch_size):
        ring = [(src, (src + k) % ch_size) for src in range(ch_size)]
        gated_parts.append(lax.ppermute(gated_out, "ch", ring))
    remote = jnp.zeros((ch_size - 1, fetched.shape[1], cols), out_weight.dtype)
    remote = lax.dynamic_update_slice_in_dim(remote, fetched, core * half, axis=2)
    remote = lax.dynamic_update_slice_in_dim(remote, swapped, (1 - core) * half, axis=2)
    weight_rows = jnp.concatenate(
        [weight_for(0, cols, 0), remote.reshape(-1, cols)], axis=0
    )
    mixed = jnp.dot(
        jnp.concatenate(gated_parts, axis=1),
        weight_rows,
        preferred_element_type=jnp.float32,
    )
    return mixed.astype(jnp.bfloat16)


def solution(mesh):
    in_specs = (
        P(("pair", "tr"), "ch"),
        P(("pair", "tr"), "ch"),
        P(("pair", "tr"), "ch"),
        P("ch", None),
        P("ch", None),
        P("ch"),
        P("ch", None),
    )
    out_specs = P(("pair", "tr"), "ch")
    return jax.shard_map(local, mesh=mesh, in_specs=in_specs, out_specs=out_specs, check_vma=False)
```

```python
import jax
import jax.numpy as jnp
from jax import lax
from jax.sharding import PartitionSpec as P

CHUNK = 128


def sequence_place():
    return lax.axis_index("pair") * lax.axis_size("tr") + lax.axis_index("tr")


def split3(values):
    first = lax.reduce_precision(values, exponent_bits=8, mantissa_bits=7)
    rest = values - first
    second = lax.reduce_precision(rest, exponent_bits=8, mantissa_bits=7)
    third = rest - second
    return (
        first.astype(jnp.bfloat16),
        second.astype(jnp.bfloat16),
        third.astype(jnp.bfloat16),
    )


def prefix_history(device_end, rate_nc, local_rows, seq_devices, seq_place):
    lag = (jnp.arange(seq_devices, dtype=jnp.int32) - 1 - seq_place).astype(jnp.float32)
    weight = jnp.where(
        lag[:, None, None] >= 0.0,
        jnp.exp(-rate_nc[None] * (local_rows * jnp.maximum(lag, 0.0))[:, None, None]),
        0.0,
    )
    return weight * device_end[None]


def chunk_ends(drive_term, rate_nc):
    local_rows, local_chan = drive_term.shape
    chunks = local_rows // CHUNK
    step = jnp.arange(CHUNK, dtype=jnp.float32)[:, None, None]
    rev = jnp.exp(-rate_nc[None] * (CHUNK - 1 - step))
    x = drive_term.reshape(chunks, CHUNK, 1, local_chan)
    return jnp.sum(x * rev[None], axis=1)


def chunk_states(ends, rate_nc):
    chunk_decay = jnp.exp(-rate_nc * CHUNK)
    local_states = []
    state = jnp.zeros_like(ends[0])
    for k in range(ends.shape[0]):
        state = chunk_decay * state + ends[k]
        local_states.append(state)
    return local_states


def local(post_gate, pre_gate, features, residues, rates, skip, out_weight):
    local_rows, local_chan = pre_gate.shape
    modes = rates.shape[1]
    chunks = local_rows // CHUNK
    seq_devices = lax.axis_size("pair") * lax.axis_size("tr")
    seq_place = sequence_place()

    early_drive = pre_gate.astype(jnp.float32) * features.astype(jnp.float32)
    early_rates = rates.T
    ends = chunk_ends(early_drive, early_rates)
    device_end = chunk_states(ends, early_rates)[-1]
    payload = prefix_history(device_end, early_rates, local_rows, seq_devices, seq_place)
    payload, out_weight, ends, pre_gate, features, rates, residues = lax.optimization_barrier(
        (payload, out_weight, ends, pre_gate, features, rates, residues)
    )
    sent = lax.all_to_all(payload, ("pair", "tr"), 0, 0, tiled=True)

    drive_term = pre_gate.astype(jnp.float32) * features.astype(jnp.float32)
    rate_nc = rates.T
    amplitude_nc = (residues * jnp.sqrt(-jnp.expm1(-2.0 * rates))).T
    step = jnp.arange(CHUNK, dtype=jnp.float32)[:, None, None]
    grow = jnp.exp(rate_nc[None] * step)
    decay = amplitude_nc[None] * jnp.exp(-rate_nc[None] * step)
    x = drive_term.reshape(chunks, CHUNK, 1, local_chan)
    scaled = (x * grow[None]).reshape(chunks, CHUNK, modes * local_chan)
    parts = split3(scaled)
    lower = (step[:, 0, 0][:, None] >= step[:, 0, 0][None, :]).astype(jnp.bfloat16)
    lower3 = jnp.concatenate([lower, lower, lower], axis=1)
    stacked = jnp.concatenate(parts, axis=1)
    cums = jnp.einsum("ji,kiz->kjz", lower3, stacked, preferred_element_type=jnp.float32)
    cums = cums.reshape(chunks, CHUNK, modes, local_chan)
    within = jnp.sum(decay[None] * cums, axis=2)
    base = within.reshape(local_rows, local_chan) + skip[None, :] * drive_term
    local_states = chunk_states(ends, rate_nc)

    base, sent = lax.optimization_barrier((base, sent))
    history = jnp.sum(sent, axis=0)
    one_step = jnp.exp(-rate_nc)
    entering = [history]
    for k in range(1, chunks):
        entering.append(local_states[k - 1] + jnp.exp(-rate_nc * (CHUNK * k)) * history)
    entering = jnp.stack(entering) * one_step[None]
    tail = decay[None, :, 0] * entering[:, None, 0]
    for n in range(1, modes):
        tail = tail + decay[None, :, n] * entering[:, None, n]
    convolved = base + tail.reshape(local_rows, local_chan)
    gated_out = (post_gate.astype(jnp.float32) * convolved).astype(jnp.bfloat16)

    ch_size = lax.axis_size("ch")
    ch_place = lax.axis_index("ch")
    core = lax.axis_index("pair")
    cols = out_weight.shape[1] // ch_size
    half = cols // 2

    def weight_for(offset, width, part):
        start = ((ch_place + offset) % ch_size) * cols + part * width
        return lax.dynamic_slice_in_dim(out_weight, start, width, axis=1)

    pieces = []
    for k in range(1, ch_size):
        ring = [(src, (src + k) % ch_size) for src in range(ch_size)]
        pieces.append(lax.ppermute(weight_for(k, half, core), "ch", ring))
    fetched = jnp.stack(pieces)
    swapped = lax.ppermute(fetched, "pair", [(0, 1), (1, 0)])
    gated_out, fetched = lax.optimization_barrier((gated_out, fetched))
    gated_parts = [gated_out]
    for k in range(1, ch_size):
        ring = [(src, (src + k) % ch_size) for src in range(ch_size)]
        gated_parts.append(lax.ppermute(gated_out, "ch", ring))
    remote = jnp.zeros((ch_size - 1, fetched.shape[1], cols), out_weight.dtype)
    remote = lax.dynamic_update_slice_in_dim(remote, fetched, core * half, axis=2)
    remote = lax.dynamic_update_slice_in_dim(remote, swapped, (1 - core) * half, axis=2)
    weight_rows = jnp.concatenate(
        [weight_for(0, cols, 0), remote.reshape(-1, cols)], axis=0
    )
    mixed = jnp.dot(
        jnp.concatenate(gated_parts, axis=1),
        weight_rows,
        preferred_element_type=jnp.float32,
    )
    return mixed.astype(jnp.bfloat16)


def solution(mesh):
    in_specs = (
        P(("pair", "tr"), "ch"),
        P(("pair", "tr"), "ch"),
        P(("pair", "tr"), "ch"),
        P("ch", None),
        P("ch", None),
        P("ch"),
        P("ch", None),
    )
    out_specs = P(("pair", "tr"), "ch")
    return jax.shard_map(local, mesh=mesh, in_specs=in_specs, out_specs=out_specs, check_vma=False)
```

```python
import jax
import jax.numpy as jnp
from jax import lax
from jax.sharding import PartitionSpec as P

CHUNK = 128


def sequence_place():
    return lax.axis_index("pair") * lax.axis_size("tr") + lax.axis_index("tr")


def split3(values):
    first = lax.reduce_precision(values, exponent_bits=8, mantissa_bits=7)
    rest = values - first
    second = lax.reduce_precision(rest, exponent_bits=8, mantissa_bits=7)
    third = rest - second
    return (
        first.astype(jnp.bfloat16),
        second.astype(jnp.bfloat16),
        third.astype(jnp.bfloat16),
    )


def prefix_history(device_end, rate_nc, local_rows, seq_devices, seq_place):
    lag = (jnp.arange(seq_devices, dtype=jnp.int32) - 1 - seq_place).astype(jnp.float32)
    weight = jnp.where(
        lag[:, None, None] >= 0.0,
        jnp.exp(-rate_nc[None] * (local_rows * jnp.maximum(lag, 0.0))[:, None, None]),
        0.0,
    )
    return weight * device_end[None]


def recurrent_convolve(pre_gate, features, residues, rates, out_weight):
    drive_term = pre_gate.astype(jnp.float32) * features.astype(jnp.float32)
    local_rows, local_chan = drive_term.shape
    modes = rates.shape[1]
    chunks = local_rows // CHUNK
    seq_devices = lax.axis_size("pair") * lax.axis_size("tr")
    seq_place = sequence_place()

    rate_nc = rates.T
    step = jnp.arange(CHUNK, dtype=jnp.float32)[:, None, None]
    rev = jnp.exp(-rate_nc[None] * (CHUNK - 1 - step))

    x = drive_term.reshape(chunks, CHUNK, 1, local_chan)
    ends = jnp.sum(x * rev[None], axis=1)
    chunk_decay = jnp.exp(-rate_nc * CHUNK)
    local_states = []
    state = jnp.zeros_like(ends[0])
    for k in range(chunks):
        state = chunk_decay * state + ends[k]
        local_states.append(state)
    payload = prefix_history(local_states[-1], rate_nc, local_rows, seq_devices, seq_place)
    payload, out_weight, ends, pre_gate, features, rates, residues = lax.optimization_barrier(
        (payload, out_weight, ends, pre_gate, features, rates, residues)
    )
    sent = lax.all_to_all(payload, ("pair", "tr"), 0, 0, tiled=True)
    drive_term = pre_gate.astype(jnp.float32) * features.astype(jnp.float32)
    x = drive_term.reshape(chunks, CHUNK, 1, local_chan)
    rate_nc = rates.T
    local_states = []
    state = jnp.zeros_like(ends[0])
    for k in range(chunks):
        state = chunk_decay * state + ends[k]
        local_states.append(state)

    amplitude_nc = (residues * jnp.sqrt(-jnp.expm1(-2.0 * rates))).T
    grow = jnp.exp(rate_nc[None] * step)
    decay = amplitude_nc[None] * jnp.exp(-rate_nc[None] * step)
    scaled = (x * grow[None]).reshape(chunks, CHUNK, modes * local_chan)
    parts = split3(scaled)
    lower = (step[:, 0, 0][:, None] >= step[:, 0, 0][None, :]).astype(jnp.bfloat16)
    lower3 = jnp.concatenate([lower, lower, lower], axis=1)
    stacked = jnp.concatenate(parts, axis=1)
    cums = jnp.einsum("ji,kiz->kjz", lower3, stacked, preferred_element_type=jnp.float32)
    cums = cums.reshape(chunks, CHUNK, modes, local_chan)
    within = jnp.sum(decay[None] * cums, axis=2)

    within, sent = lax.optimization_barrier((within, sent))
    history = jnp.sum(sent, axis=0)
    one_step = jnp.exp(-rate_nc)
    entering = [history]
    for k in range(1, chunks):
        entering.append(local_states[k - 1] + jnp.exp(-rate_nc * (CHUNK * k)) * history)
    entering = jnp.stack(entering) * one_step[None]
    convolved = within + jnp.sum(decay[None] * entering[:, None], axis=2)
    return convolved.reshape(local_rows, local_chan), out_weight, drive_term


def local(post_gate, pre_gate, features, residues, rates, skip, out_weight):
    convolved, out_weight, drive_term = recurrent_convolve(pre_gate, features, residues, rates, out_weight)
    gated_out = (post_gate.astype(jnp.float32) * (convolved + skip[None, :] * drive_term)).astype(
        jnp.bfloat16
    )
    ch_size = lax.axis_size("ch")
    ch_place = lax.axis_index("ch")
    core = lax.axis_index("pair")
    cols = out_weight.shape[1] // ch_size
    half = cols // 2

    def weight_for(offset, width, part):
        start = ((ch_place + offset) % ch_size) * cols + part * width
        return lax.dynamic_slice_in_dim(out_weight, start, width, axis=1)

    pieces = []
    for k in range(1, ch_size):
        ring = [(src, (src + k) % ch_size) for src in range(ch_size)]
        pieces.append(lax.ppermute(weight_for(k, half, core), "ch", ring))
    fetched = jnp.stack(pieces)
    swapped = lax.ppermute(fetched, "pair", [(0, 1), (1, 0)])
    gated_out, fetched = lax.optimization_barrier((gated_out, fetched))
    received = {}
    for k in sorted(range(1, ch_size), key=lambda k: -min(k, ch_size - k)):
        ring = [(src, (src + k) % ch_size) for src in range(ch_size)]
        received[k] = lax.ppermute(gated_out, "ch", ring)
    gated_parts = [gated_out] + [received[k] for k in range(1, ch_size)]
    remote = jnp.zeros((ch_size - 1, fetched.shape[1], cols), out_weight.dtype)
    remote = lax.dynamic_update_slice_in_dim(remote, fetched, core * half, axis=2)
    remote = lax.dynamic_update_slice_in_dim(remote, swapped, (1 - core) * half, axis=2)
    weight_rows = jnp.concatenate(
        [weight_for(0, cols, 0), remote.reshape(-1, cols)], axis=0
    )
    mixed = jnp.dot(
        jnp.concatenate(gated_parts, axis=1),
        weight_rows,
        preferred_element_type=jnp.float32,
    )
    return mixed.astype(jnp.bfloat16)


def solution(mesh):
    in_specs = (
        P(("pair", "tr"), "ch"),
        P(("pair", "tr"), "ch"),
        P(("pair", "tr"), "ch"),
        P("ch", None),
        P("ch", None),
        P("ch"),
        P("ch", None),
    )
    out_specs = P(("pair", "tr"), "ch")
    return jax.shard_map(local, mesh=mesh, in_specs=in_specs, out_specs=out_specs, check_vma=False)
```

```python
import jax
import jax.numpy as jnp
from jax import lax
from jax.sharding import PartitionSpec as P

CHUNK = 128


def sequence_place():
    return lax.axis_index("pair") * lax.axis_size("tr") + lax.axis_index("tr")


def split3(values):
    first = lax.reduce_precision(values, exponent_bits=8, mantissa_bits=7)
    rest = values - first
    second = lax.reduce_precision(rest, exponent_bits=8, mantissa_bits=7)
    third = rest - second
    return (
        first.astype(jnp.bfloat16),
        second.astype(jnp.bfloat16),
        third.astype(jnp.bfloat16),
    )


def state_of(pre_gate, features, rate_nc):
    drive_term = pre_gate.astype(jnp.float32) * features.astype(jnp.float32)
    local_rows, local_chan = drive_term.shape
    chunks = local_rows // CHUNK
    step = jnp.arange(CHUNK, dtype=jnp.float32)[:, None, None]
    rev = jnp.exp(-rate_nc[None] * (CHUNK - 1 - step))
    x = drive_term.reshape(chunks, CHUNK, 1, local_chan)
    ends = jnp.sum(x * rev[None], axis=1)
    chunk_decay = jnp.exp(-rate_nc * CHUNK)
    state = jnp.zeros_like(ends[0])
    for k in range(chunks):
        state = chunk_decay * state + ends[k]
    return ends, state


def history_payload(own_end, partner_end, rate_nc, local_rows):
    tr_size = lax.axis_size("tr")
    tr_place = lax.axis_index("tr")
    second_core = (lax.axis_index("pair") == 1).astype(jnp.float32)
    target = jnp.arange(tr_size, dtype=jnp.int32)
    lag = (target - 1 - tr_place).astype(jnp.float32)
    own_weight = jnp.where(
        lag[:, None, None] >= 0.0,
        jnp.exp(-rate_nc[None] * (local_rows * jnp.maximum(lag, 0.0))[:, None, None]),
        0.0,
    )
    partner_lag = lag + tr_size
    partner_weight = second_core * jnp.exp(
        -rate_nc[None] * (local_rows * partner_lag)[:, None, None]
    )
    return own_weight * own_end[None] + partner_weight * partner_end[None]


def recurrent_convolve(pre_gate, features, residues, rates, out_weight):
    local_rows, local_chan = pre_gate.shape
    modes = rates.shape[1]
    chunks = local_rows // CHUNK
    seq_devices = lax.axis_size("pair") * lax.axis_size("tr")
    seq_place = sequence_place()

    rate_nc = rates.T
    step = jnp.arange(CHUNK, dtype=jnp.float32)[:, None, None]
    chunk_decay = jnp.exp(-rate_nc * CHUNK)
    partner = lax.ppermute(jnp.stack([pre_gate, features]), "pair", [(0, 1), (1, 0)])
    ends, own_end = state_of(pre_gate, features, rate_nc)
    _, partner_end = state_of(partner[0], partner[1], rate_nc)
    payload = history_payload(own_end, partner_end, rate_nc, local_rows)
    payload, out_weight, ends, pre_gate, features, rates, residues = lax.optimization_barrier(
        (payload, out_weight, ends, pre_gate, features, rates, residues)
    )
    sent = lax.all_to_all(payload, "tr", 0, 0, tiled=True)
    drive_term = pre_gate.astype(jnp.float32) * features.astype(jnp.float32)
    x = drive_term.reshape(chunks, CHUNK, 1, local_chan)
    rate_nc = rates.T
    local_states = []
    state = jnp.zeros_like(ends[0])
    for k in range(chunks):
        state = chunk_decay * state + ends[k]
        local_states.append(state)

    amplitude_nc = (residues * jnp.sqrt(-jnp.expm1(-2.0 * rates))).T
    grow = jnp.exp(rate_nc[None] * step)
    decay = amplitude_nc[None] * jnp.exp(-rate_nc[None] * step)
    scaled = (x * grow[None]).reshape(chunks, CHUNK, modes * local_chan)
    parts = split3(scaled)
    lower = (step[:, 0, 0][:, None] >= step[:, 0, 0][None, :]).astype(jnp.bfloat16)
    lower3 = jnp.concatenate([lower, lower, lower], axis=1)
    stacked = jnp.concatenate(parts, axis=1)
    cums = jnp.einsum("ji,kiz->kjz", lower3, stacked, preferred_element_type=jnp.float32)
    cums = cums.reshape(chunks, CHUNK, modes, local_chan)
    within = jnp.sum(decay[None] * cums, axis=2)

    within, sent = lax.optimization_barrier((within, sent))
    history = jnp.sum(sent, axis=0)
    one_step = jnp.exp(-rate_nc)
    entering = [history]
    for k in range(1, chunks):
        entering.append(local_states[k - 1] + jnp.exp(-rate_nc * (CHUNK * k)) * history)
    entering = jnp.stack(entering) * one_step[None]
    convolved = within + jnp.sum(decay[None] * entering[:, None], axis=2)
    return convolved.reshape(local_rows, local_chan), out_weight, drive_term


def local(post_gate, pre_gate, features, residues, rates, skip, out_weight):
    convolved, out_weight, drive_term = recurrent_convolve(pre_gate, features, residues, rates, out_weight)
    gated_out = (post_gate.astype(jnp.float32) * (convolved + skip[None, :] * drive_term)).astype(
        jnp.bfloat16
    )
    ch_size = lax.axis_size("ch")
    ch_place = lax.axis_index("ch")
    core = lax.axis_index("pair")
    cols = out_weight.shape[1] // ch_size
    half = cols // 2

    def weight_for(offset, width, part):
        start = ((ch_place + offset) % ch_size) * cols + part * width
        return lax.dynamic_slice_in_dim(out_weight, start, width, axis=1)

    pieces = []
    for k in range(1, ch_size):
        ring = [(src, (src + k) % ch_size) for src in range(ch_size)]
        pieces.append(lax.ppermute(weight_for(k, half, core), "ch", ring))
    fetched = jnp.stack(pieces)
    swapped = lax.ppermute(fetched, "pair", [(0, 1), (1, 0)])
    gated_out, fetched = lax.optimization_barrier((gated_out, fetched))
    received = {}
    for k in sorted(range(1, ch_size), key=lambda k: -min(k, ch_size - k)):
        ring = [(src, (src + k) % ch_size) for src in range(ch_size)]
        received[k] = lax.ppermute(gated_out, "ch", ring)
    gated_parts = [gated_out] + [received[k] for k in range(1, ch_size)]
    remote = jnp.zeros((ch_size - 1, fetched.shape[1], cols), out_weight.dtype)
    remote = lax.dynamic_update_slice_in_dim(remote, fetched, core * half, axis=2)
    remote = lax.dynamic_update_slice_in_dim(remote, swapped, (1 - core) * half, axis=2)
    weight_rows = jnp.concatenate(
        [weight_for(0, cols, 0), remote.reshape(-1, cols)], axis=0
    )
    mixed = jnp.dot(
        jnp.concatenate(gated_parts, axis=1),
        weight_rows,
        preferred_element_type=jnp.float32,
    )
    return mixed.astype(jnp.bfloat16)


def solution(mesh):
    in_specs = (
        P(("pair", "tr"), "ch"),
        P(("pair", "tr"), "ch"),
        P(("pair", "tr"), "ch"),
        P("ch", None),
        P("ch", None),
        P("ch"),
        P("ch", None),
    )
    out_specs = P(("pair", "tr"), "ch")
    return jax.shard_map(local, mesh=mesh, in_specs=in_specs, out_specs=out_specs, check_vma=False)
```

```python
import jax
import jax.numpy as jnp
from jax import lax
from jax.sharding import PartitionSpec as P

CHUNK = 128


def sequence_place():
    return lax.axis_index("pair") * lax.axis_size("tr") + lax.axis_index("tr")


def split3(values):
    first = lax.reduce_precision(values, exponent_bits=8, mantissa_bits=7)
    rest = values - first
    second = lax.reduce_precision(rest, exponent_bits=8, mantissa_bits=7)
    third = rest - second
    return (
        first.astype(jnp.bfloat16),
        second.astype(jnp.bfloat16),
        third.astype(jnp.bfloat16),
    )


def state_of(pre_gate, features, rate_nc):
    drive_term = pre_gate.astype(jnp.float32) * features.astype(jnp.float32)
    local_rows, local_chan = drive_term.shape
    chunks = local_rows // CHUNK
    step = jnp.arange(CHUNK, dtype=jnp.float32)[:, None, None]
    rev = jnp.exp(-rate_nc[None] * (CHUNK - 1 - step))
    x = drive_term.reshape(chunks, CHUNK, 1, local_chan)
    ends = jnp.sum(x * rev[None], axis=1)
    chunk_decay = jnp.exp(-rate_nc * CHUNK)
    state = jnp.zeros_like(ends[0])
    for k in range(chunks):
        state = chunk_decay * state + ends[k]
    return ends, state


def history_payload(own_end, partner_end, rate_nc, local_rows):
    tr_size = lax.axis_size("tr")
    tr_place = lax.axis_index("tr")
    second_core = (lax.axis_index("pair") == 1).astype(jnp.float32)
    target = jnp.arange(tr_size, dtype=jnp.int32)
    lag = (target - 1 - tr_place).astype(jnp.float32)
    own_weight = jnp.where(
        lag[:, None, None] >= 0.0,
        jnp.exp(-rate_nc[None] * (local_rows * jnp.maximum(lag, 0.0))[:, None, None]),
        0.0,
    )
    partner_lag = lag + tr_size
    partner_weight = second_core * jnp.exp(
        -rate_nc[None] * (local_rows * partner_lag)[:, None, None]
    )
    return own_weight * own_end[None] + partner_weight * partner_end[None]


def recurrent_convolve(pre_gate, features, residues, rates, out_weight):
    local_rows, local_chan = pre_gate.shape
    modes = rates.shape[1]
    chunks = local_rows // CHUNK
    seq_devices = lax.axis_size("pair") * lax.axis_size("tr")
    seq_place = sequence_place()

    rate_nc = rates.T
    step = jnp.arange(CHUNK, dtype=jnp.float32)[:, None, None]
    chunk_decay = jnp.exp(-rate_nc * CHUNK)
    partner = lax.ppermute(jnp.stack([pre_gate, features]), "pair", [(0, 1), (1, 0)])
    ends, own_end = state_of(pre_gate, features, rate_nc)
    _, partner_end = state_of(partner[0], partner[1], rate_nc)
    payload = history_payload(own_end, partner_end, rate_nc, local_rows)
    payload, out_weight, ends, pre_gate, features, rates, residues = lax.optimization_barrier(
        (payload, out_weight, ends, pre_gate, features, rates, residues)
    )
    sent = lax.all_to_all(payload, "tr", 0, 0, tiled=True)
    drive_term = pre_gate.astype(jnp.float32) * features.astype(jnp.float32)
    x = drive_term.reshape(chunks, CHUNK, 1, local_chan)
    rate_nc = rates.T
    local_states = []
    state = jnp.zeros_like(ends[0])
    for k in range(chunks):
        state = chunk_decay * state + ends[k]
        local_states.append(state)

    amplitude_nc = (residues * jnp.sqrt(-jnp.expm1(-2.0 * rates))).T
    grow = jnp.exp(rate_nc[None] * step)
    decay = amplitude_nc[None] * jnp.exp(-rate_nc[None] * step)
    scaled = (x * grow[None]).reshape(chunks, CHUNK, modes * local_chan)
    parts = split3(scaled)
    lower = (step[:, 0, 0][:, None] >= step[:, 0, 0][None, :]).astype(jnp.bfloat16)
    lower3 = jnp.concatenate([lower, lower, lower], axis=1)
    stacked = jnp.concatenate(parts, axis=1)
    cums = jnp.einsum("ji,kiz->kjz", lower3, stacked, preferred_element_type=jnp.float32)
    cums = cums.reshape(chunks, CHUNK, modes, local_chan)
    within = jnp.sum(decay[None] * cums, axis=2)

    within, sent = lax.optimization_barrier((within, sent))
    history = jnp.sum(sent, axis=0)
    one_step = jnp.exp(-rate_nc)
    entering = [history]
    for k in range(1, chunks):
        entering.append(local_states[k - 1] + jnp.exp(-rate_nc * (CHUNK * k)) * history)
    entering = jnp.stack(entering) * one_step[None]
    convolved = within + jnp.sum(decay[None] * entering[:, None], axis=2)
    return convolved.reshape(local_rows, local_chan), out_weight, drive_term


def local(post_gate, pre_gate, features, residues, rates, skip, out_weight):
    convolved, out_weight, drive_term = recurrent_convolve(pre_gate, features, residues, rates, out_weight)
    gated_out = (post_gate.astype(jnp.float32) * (convolved + skip[None, :] * drive_term)).astype(
        jnp.bfloat16
    )
    ch_size = lax.axis_size("ch")
    ch_place = lax.axis_index("ch")
    core = lax.axis_index("pair")
    cols = out_weight.shape[1] // ch_size
    half = cols // 2

    def weight_for(offset, width, part):
        start = ((ch_place + offset) % ch_size) * cols + part * width
        return lax.dynamic_slice_in_dim(out_weight, start, width, axis=1)

    if ch_size == 4:
        quarter = half // 2
        far = weight_for(2, half, core)
        up_ring = [(src, (src + 1) % ch_size) for src in range(ch_size)]
        down_ring = [(src, (src - 1) % ch_size) for src in range(ch_size)]
        up = lax.ppermute(
            jnp.concatenate([weight_for(1, half, core), far[:, :quarter]], axis=1), "ch", up_ring
        )
        down = lax.ppermute(
            jnp.concatenate([weight_for(3, half, core), far[:, quarter:]], axis=1), "ch", down_ring
        )
        relay_up = lax.ppermute(up[:, half:], "ch", up_ring)
        relay_down = lax.ppermute(down[:, half:], "ch", down_ring)
        pieces = [up[:, :half], jnp.concatenate([relay_up, relay_down], axis=1), down[:, :half]]
    else:
        pieces = []
        for k in range(1, ch_size):
            ring = [(src, (src + k) % ch_size) for src in range(ch_size)]
            pieces.append(lax.ppermute(weight_for(k, half, core), "ch", ring))
    fetched = jnp.stack(pieces)
    swapped = lax.ppermute(fetched, "pair", [(0, 1), (1, 0)])
    gated_out, fetched = lax.optimization_barrier((gated_out, fetched))
    received = {}
    for k in sorted(range(1, ch_size), key=lambda k: -min(k, ch_size - k)):
        ring = [(src, (src + k) % ch_size) for src in range(ch_size)]
        received[k] = lax.ppermute(gated_out, "ch", ring)
    gated_parts = [gated_out] + [received[k] for k in range(1, ch_size)]
    remote = jnp.zeros((ch_size - 1, fetched.shape[1], cols), out_weight.dtype)
    remote = lax.dynamic_update_slice_in_dim(remote, fetched, core * half, axis=2)
    remote = lax.dynamic_update_slice_in_dim(remote, swapped, (1 - core) * half, axis=2)
    weight_rows = jnp.concatenate(
        [weight_for(0, cols, 0), remote.reshape(-1, cols)], axis=0
    )
    mixed = jnp.dot(
        jnp.concatenate(gated_parts, axis=1),
        weight_rows,
        preferred_element_type=jnp.float32,
    )
    return mixed.astype(jnp.bfloat16)


def solution(mesh):
    in_specs = (
        P(("pair", "tr"), "ch"),
        P(("pair", "tr"), "ch"),
        P(("pair", "tr"), "ch"),
        P("ch", None),
        P("ch", None),
        P("ch"),
        P("ch", None),
    )
    out_specs = P(("pair", "tr"), "ch")
    return jax.shard_map(local, mesh=mesh, in_specs=in_specs, out_specs=out_specs, check_vma=False)
```

```python
import jax
import jax.numpy as jnp
from jax import lax
from jax.sharding import PartitionSpec as P

CHUNK = 128


def sequence_place():
    return lax.axis_index("pair") * lax.axis_size("tr") + lax.axis_index("tr")


def split3(values):
    first = lax.reduce_precision(values, exponent_bits=8, mantissa_bits=7)
    rest = values - first
    second = lax.reduce_precision(rest, exponent_bits=8, mantissa_bits=7)
    third = rest - second
    return (
        first.astype(jnp.bfloat16),
        second.astype(jnp.bfloat16),
        third.astype(jnp.bfloat16),
    )


def state_of(pre_gate, features, rate_nc):
    drive_term = pre_gate.astype(jnp.float32) * features.astype(jnp.float32)
    local_rows, local_chan = drive_term.shape
    chunks = local_rows // CHUNK
    step = jnp.arange(CHUNK, dtype=jnp.float32)[:, None, None]
    rev = jnp.exp(-rate_nc[None] * (CHUNK - 1 - step))
    x = drive_term.reshape(chunks, CHUNK, 1, local_chan)
    ends = jnp.sum(x * rev[None], axis=1)
    chunk_decay = jnp.exp(-rate_nc * CHUNK)
    state = jnp.zeros_like(ends[0])
    for k in range(chunks):
        state = chunk_decay * state + ends[k]
    return ends, state


def history_payload(own_end, partner_end, rate_nc, local_rows):
    tr_size = lax.axis_size("tr")
    tr_place = lax.axis_index("tr")
    second_core = (lax.axis_index("pair") == 1).astype(jnp.float32)
    target = jnp.arange(tr_size, dtype=jnp.int32)
    lag = (target - 1 - tr_place).astype(jnp.float32)
    own_weight = jnp.where(
        lag[:, None, None] >= 0.0,
        jnp.exp(-rate_nc[None] * (local_rows * jnp.maximum(lag, 0.0))[:, None, None]),
        0.0,
    )
    partner_lag = lag + tr_size
    partner_weight = second_core * jnp.exp(
        -rate_nc[None] * (local_rows * partner_lag)[:, None, None]
    )
    return own_weight * own_end[None] + partner_weight * partner_end[None]


def recurrent_convolve(pre_gate, features, residues, rates, out_weight):
    local_rows, local_chan = pre_gate.shape
    modes = rates.shape[1]
    chunks = local_rows // CHUNK
    seq_devices = lax.axis_size("pair") * lax.axis_size("tr")
    seq_place = sequence_place()

    rate_nc = rates.T
    step = jnp.arange(CHUNK, dtype=jnp.float32)[:, None, None]
    chunk_decay = jnp.exp(-rate_nc * CHUNK)
    partner = lax.ppermute(jnp.stack([pre_gate, features]), "pair", [(0, 1), (1, 0)])
    ends, own_end = state_of(pre_gate, features, rate_nc)
    _, partner_end = state_of(partner[0], partner[1], rate_nc)
    payload = history_payload(own_end, partner_end, rate_nc, local_rows)
    payload, out_weight, ends, pre_gate, features, rates, residues = lax.optimization_barrier(
        (payload, out_weight, ends, pre_gate, features, rates, residues)
    )
    sent = lax.all_to_all(payload, "tr", 0, 0, tiled=True)
    drive_term = pre_gate.astype(jnp.float32) * features.astype(jnp.float32)
    x = drive_term.reshape(chunks, CHUNK, 1, local_chan)
    rate_nc = rates.T
    local_states = []
    state = jnp.zeros_like(ends[0])
    for k in range(chunks):
        state = chunk_decay * state + ends[k]
        local_states.append(state)

    amplitude_nc = (residues * jnp.sqrt(-jnp.expm1(-2.0 * rates))).T
    grow = jnp.exp(rate_nc[None] * step)
    decay = amplitude_nc[None] * jnp.exp(-rate_nc[None] * step)
    scaled = (x * grow[None]).reshape(chunks, CHUNK, modes * local_chan)
    parts = split3(scaled)
    lower = (step[:, 0, 0][:, None] >= step[:, 0, 0][None, :]).astype(jnp.bfloat16)
    lower3 = jnp.concatenate([lower, lower, lower], axis=1)
    stacked = jnp.concatenate(parts, axis=1)
    cums = jnp.einsum("ji,kiz->kjz", lower3, stacked, preferred_element_type=jnp.float32)
    cums = cums.reshape(chunks, CHUNK, modes, local_chan)
    within = jnp.sum(decay[None] * cums, axis=2)

    within, sent = lax.optimization_barrier((within, sent))
    history = jnp.sum(sent, axis=0)
    one_step = jnp.exp(-rate_nc)
    entering = [history]
    for k in range(1, chunks):
        entering.append(local_states[k - 1] + jnp.exp(-rate_nc * (CHUNK * k)) * history)
    entering = jnp.stack(entering) * one_step[None]
    convolved = within + jnp.sum(decay[None] * entering[:, None], axis=2)
    return convolved.reshape(local_rows, local_chan), out_weight, drive_term


def local(post_gate, pre_gate, features, residues, rates, skip, out_weight):
    convolved, out_weight, drive_term = recurrent_convolve(pre_gate, features, residues, rates, out_weight)
    gated_out = (post_gate.astype(jnp.float32) * (convolved + skip[None, :] * drive_term)).astype(
        jnp.bfloat16
    )
    ch_size = lax.axis_size("ch")
    ch_place = lax.axis_index("ch")
    core = lax.axis_index("pair")
    cols = out_weight.shape[1] // ch_size
    half = cols // 2

    def weight_for(offset, width, part):
        start = ((ch_place + offset) % ch_size) * cols + part * width
        return lax.dynamic_slice_in_dim(out_weight, start, width, axis=1)

    pieces = []
    for k in range(1, ch_size):
        ring = [(src, (src + k) % ch_size) for src in range(ch_size)]
        pieces.append(lax.ppermute(weight_for(k, half, core), "ch", ring))
    gated_out, *pieces = lax.optimization_barrier((gated_out, *pieces))
    fetched = jnp.stack(pieces)
    swapped = lax.ppermute(fetched, "pair", [(0, 1), (1, 0)])
    received = {}
    for k in sorted(range(1, ch_size), key=lambda k: -min(k, ch_size - k)):
        ring = [(src, (src + k) % ch_size) for src in range(ch_size)]
        received[k] = lax.ppermute(gated_out, "ch", ring)
    gated_parts = [gated_out] + [received[k] for k in range(1, ch_size)]
    remote = jnp.zeros((ch_size - 1, fetched.shape[1], cols), out_weight.dtype)
    remote = lax.dynamic_update_slice_in_dim(remote, fetched, core * half, axis=2)
    remote = lax.dynamic_update_slice_in_dim(remote, swapped, (1 - core) * half, axis=2)
    weight_rows = jnp.concatenate(
        [weight_for(0, cols, 0), remote.reshape(-1, cols)], axis=0
    )
    mixed = jnp.dot(
        jnp.concatenate(gated_parts, axis=1),
        weight_rows,
        preferred_element_type=jnp.float32,
    )
    return mixed.astype(jnp.bfloat16)


def solution(mesh):
    in_specs = (
        P(("pair", "tr"), "ch"),
        P(("pair", "tr"), "ch"),
        P(("pair", "tr"), "ch"),
        P("ch", None),
        P("ch", None),
        P("ch"),
        P("ch", None),
    )
    out_specs = P(("pair", "tr"), "ch")
    return jax.shard_map(local, mesh=mesh, in_specs=in_specs, out_specs=out_specs, check_vma=False)
```

```python
import jax
import jax.numpy as jnp
from jax import lax
from jax.sharding import PartitionSpec as P

CHUNK = 128


def sequence_place():
    return lax.axis_index("pair") * lax.axis_size("tr") + lax.axis_index("tr")


def split3(values):
    first = lax.reduce_precision(values, exponent_bits=8, mantissa_bits=7)
    rest = values - first
    second = lax.reduce_precision(rest, exponent_bits=8, mantissa_bits=7)
    third = rest - second
    return (
        first.astype(jnp.bfloat16),
        second.astype(jnp.bfloat16),
        third.astype(jnp.bfloat16),
    )


def state_of(pre_gate, features, rate_nc):
    drive_term = pre_gate.astype(jnp.float32) * features.astype(jnp.float32)
    local_rows, local_chan = drive_term.shape
    chunks = local_rows // CHUNK
    step = jnp.arange(CHUNK, dtype=jnp.float32)[:, None, None]
    rev = jnp.exp(-rate_nc[None] * (CHUNK - 1 - step))
    x = drive_term.reshape(chunks, CHUNK, 1, local_chan)
    ends = jnp.sum(x * rev[None], axis=1)
    chunk_decay = jnp.exp(-rate_nc * CHUNK)
    state = jnp.zeros_like(ends[0])
    for k in range(chunks):
        state = chunk_decay * state + ends[k]
    return ends, state


def history_payload(own_end, partner_end, rate_nc, local_rows):
    tr_size = lax.axis_size("tr")
    tr_place = lax.axis_index("tr")
    second_core = (lax.axis_index("pair") == 1).astype(jnp.float32)
    target = jnp.arange(tr_size, dtype=jnp.int32)
    lag = (target - 1 - tr_place).astype(jnp.float32)
    own_weight = jnp.where(
        lag[:, None, None] >= 0.0,
        jnp.exp(-rate_nc[None] * (local_rows * jnp.maximum(lag, 0.0))[:, None, None]),
        0.0,
    )
    partner_lag = lag + tr_size
    partner_weight = second_core * jnp.exp(
        -rate_nc[None] * (local_rows * partner_lag)[:, None, None]
    )
    return own_weight * own_end[None] + partner_weight * partner_end[None]


def recurrent_convolve(pre_gate, features, residues, rates, out_weight):
    local_rows, local_chan = pre_gate.shape
    modes = rates.shape[1]
    chunks = local_rows // CHUNK
    seq_devices = lax.axis_size("pair") * lax.axis_size("tr")
    seq_place = sequence_place()

    rate_nc = rates.T
    step = jnp.arange(CHUNK, dtype=jnp.float32)[:, None, None]
    chunk_decay = jnp.exp(-rate_nc * CHUNK)
    partner = lax.ppermute(jnp.stack([pre_gate, features]), "pair", [(0, 1), (1, 0)])
    ends, own_end = state_of(pre_gate, features, rate_nc)
    _, partner_end = state_of(partner[0], partner[1], rate_nc)
    payload = history_payload(own_end, partner_end, rate_nc, local_rows)
    payload, out_weight, ends, pre_gate, features, rates, residues = lax.optimization_barrier(
        (payload, out_weight, ends, pre_gate, features, rates, residues)
    )
    sent = lax.all_to_all(payload, "tr", 0, 0, tiled=True)
    drive_term = pre_gate.astype(jnp.float32) * features.astype(jnp.float32)
    x = drive_term.reshape(chunks, CHUNK, 1, local_chan)
    rate_nc = rates.T
    local_states = []
    state = jnp.zeros_like(ends[0])
    for k in range(chunks):
        state = chunk_decay * state + ends[k]
        local_states.append(state)

    amplitude_nc = (residues * jnp.sqrt(-jnp.expm1(-2.0 * rates))).T
    grow = jnp.exp(rate_nc[None] * step)
    decay = amplitude_nc[None] * jnp.exp(-rate_nc[None] * step)
    scaled = (x * grow[None]).reshape(chunks, CHUNK, modes * local_chan)
    parts = split3(scaled)
    lower = (step[:, 0, 0][:, None] >= step[:, 0, 0][None, :]).astype(jnp.bfloat16)
    lower3 = jnp.concatenate([lower, lower, lower], axis=1)
    stacked = jnp.concatenate(parts, axis=1)
    cums = jnp.einsum("ji,kiz->kjz", lower3, stacked, preferred_element_type=jnp.float32)
    cums = cums.reshape(chunks, CHUNK, modes, local_chan)
    within = jnp.sum(decay[None] * cums, axis=2)

    within, sent = lax.optimization_barrier((within, sent))
    history = jnp.sum(sent, axis=0)
    one_step = jnp.exp(-rate_nc)
    entering = [history]
    for k in range(1, chunks):
        entering.append(local_states[k - 1] + jnp.exp(-rate_nc * (CHUNK * k)) * history)
    entering = jnp.stack(entering) * one_step[None]
    convolved = within + jnp.sum(decay[None] * entering[:, None], axis=2)
    return convolved.reshape(local_rows, local_chan), out_weight, drive_term


def local(post_gate, pre_gate, features, residues, rates, skip, out_weight):
    convolved, out_weight, drive_term = recurrent_convolve(pre_gate, features, residues, rates, out_weight)
    gated_out = (post_gate.astype(jnp.float32) * (convolved + skip[None, :] * drive_term)).astype(
        jnp.bfloat16
    )
    ch_size = lax.axis_size("ch")
    ch_place = lax.axis_index("ch")
    core = lax.axis_index("pair")
    cols = out_weight.shape[1] // ch_size
    half = cols // 2

    def weight_for(offset, width, part):
        start = ((ch_place + offset) % ch_size) * cols + part * width
        return lax.dynamic_slice_in_dim(out_weight, start, width, axis=1)

    pieces = []
    for k in range(1, ch_size):
        ring = [(src, (src + k) % ch_size) for src in range(ch_size)]
        pieces.append(lax.ppermute(weight_for(k, half, core), "ch", ring))
    received = {}
    for k in sorted(range(1, ch_size), key=lambda k: -min(k, ch_size - k)):
        ring = [(src, (src + k) % ch_size) for src in range(ch_size)]
        received[k] = lax.ppermute(gated_out, "ch", ring)
    received[1], *pieces = lax.optimization_barrier((received[1], *pieces))
    fetched = jnp.stack(pieces)
    swapped = lax.ppermute(fetched, "pair", [(0, 1), (1, 0)])
    gated_parts = [gated_out] + [received[k] for k in range(1, ch_size)]
    remote = jnp.zeros((ch_size - 1, fetched.shape[1], cols), out_weight.dtype)
    remote = lax.dynamic_update_slice_in_dim(remote, fetched, core * half, axis=2)
    remote = lax.dynamic_update_slice_in_dim(remote, swapped, (1 - core) * half, axis=2)
    weight_rows = jnp.concatenate(
        [weight_for(0, cols, 0), remote.reshape(-1, cols)], axis=0
    )
    mixed = jnp.dot(
        jnp.concatenate(gated_parts, axis=1),
        weight_rows,
        preferred_element_type=jnp.float32,
    )
    return mixed.astype(jnp.bfloat16)


def solution(mesh):
    in_specs = (
        P(("pair", "tr"), "ch"),
        P(("pair", "tr"), "ch"),
        P(("pair", "tr"), "ch"),
        P("ch", None),
        P("ch", None),
        P("ch"),
        P("ch", None),
    )
    out_specs = P(("pair", "tr"), "ch")
    return jax.shard_map(local, mesh=mesh, in_specs=in_specs, out_specs=out_specs, check_vma=False)
```

```python
import jax
import jax.numpy as jnp
from jax import lax
from jax.sharding import PartitionSpec as P

CHUNK = 128


def sequence_place():
    return lax.axis_index("pair") * lax.axis_size("tr") + lax.axis_index("tr")


def split3(values):
    first = lax.reduce_precision(values, exponent_bits=8, mantissa_bits=7)
    rest = values - first
    second = lax.reduce_precision(rest, exponent_bits=8, mantissa_bits=7)
    third = rest - second
    return (
        first.astype(jnp.bfloat16),
        second.astype(jnp.bfloat16),
        third.astype(jnp.bfloat16),
    )


def state_of(pre_gate, features, rate_nc):
    drive_term = pre_gate.astype(jnp.float32) * features.astype(jnp.float32)
    local_rows, local_chan = drive_term.shape
    chunks = local_rows // CHUNK
    step = jnp.arange(CHUNK, dtype=jnp.float32)[:, None, None]
    rev = jnp.exp(-rate_nc[None] * (CHUNK - 1 - step))
    x = drive_term.reshape(chunks, CHUNK, 1, local_chan)
    ends = jnp.sum(x * rev[None], axis=1)
    chunk_decay = jnp.exp(-rate_nc * CHUNK)
    state = jnp.zeros_like(ends[0])
    for k in range(chunks):
        state = chunk_decay * state + ends[k]
    return ends, state


def history_payload(own_end, partner_end, rate_nc, local_rows):
    tr_size = lax.axis_size("tr")
    tr_place = lax.axis_index("tr")
    second_core = (lax.axis_index("pair") == 1).astype(jnp.float32)
    target = jnp.arange(tr_size, dtype=jnp.int32)
    lag = (target - 1 - tr_place).astype(jnp.float32)
    own_weight = jnp.where(
        lag[:, None, None] >= 0.0,
        jnp.exp(-rate_nc[None] * (local_rows * jnp.maximum(lag, 0.0))[:, None, None]),
        0.0,
    )
    partner_lag = lag + tr_size
    partner_weight = second_core * jnp.exp(
        -rate_nc[None] * (local_rows * partner_lag)[:, None, None]
    )
    return own_weight * own_end[None] + partner_weight * partner_end[None]


def recurrent_convolve(pre_gate, features, residues, rates, out_weight):
    local_rows, local_chan = pre_gate.shape
    modes = rates.shape[1]
    chunks = local_rows // CHUNK
    seq_devices = lax.axis_size("pair") * lax.axis_size("tr")
    seq_place = sequence_place()

    rate_nc = rates.T
    step = jnp.arange(CHUNK, dtype=jnp.float32)[:, None, None]
    chunk_decay = jnp.exp(-rate_nc * CHUNK)
    partner = lax.ppermute(jnp.stack([pre_gate, features]), "pair", [(0, 1), (1, 0)])
    ends, own_end = state_of(pre_gate, features, rate_nc)
    _, partner_end = state_of(partner[0], partner[1], rate_nc)
    payload = history_payload(own_end, partner_end, rate_nc, local_rows)
    payload, out_weight, ends, pre_gate, features, rates, residues = lax.optimization_barrier(
        (payload, out_weight, ends, pre_gate, features, rates, residues)
    )
    sent = lax.all_to_all(payload, "tr", 0, 0, tiled=True)
    drive_term = pre_gate.astype(jnp.float32) * features.astype(jnp.float32)
    x = drive_term.reshape(chunks, CHUNK, 1, local_chan)
    rate_nc = rates.T
    local_states = []
    state = jnp.zeros_like(ends[0])
    for k in range(chunks):
        state = chunk_decay * state + ends[k]
        local_states.append(state)

    amplitude_nc = (residues * jnp.sqrt(-jnp.expm1(-2.0 * rates))).T
    grow = jnp.exp(rate_nc[None] * step)
    decay = amplitude_nc[None] * jnp.exp(-rate_nc[None] * step)
    scaled = (x * grow[None]).reshape(chunks, CHUNK, modes * local_chan)
    parts = split3(scaled)
    lower = (step[:, 0, 0][:, None] >= step[:, 0, 0][None, :]).astype(jnp.bfloat16)
    lower3 = jnp.concatenate([lower, lower, lower], axis=1)
    stacked = jnp.concatenate(parts, axis=1)
    cums = jnp.einsum("ji,kiz->kjz", lower3, stacked, preferred_element_type=jnp.float32)
    cums = cums.reshape(chunks, CHUNK, modes, local_chan)
    within = jnp.sum(decay[None] * cums, axis=2)

    ch_size = lax.axis_size("ch")
    cols = out_weight.shape[1] // ch_size
    own_cols = lax.dynamic_slice_in_dim(out_weight, lax.axis_index("ch") * cols, cols, axis=1)
    within, sent, own_cols = lax.optimization_barrier((within, sent, own_cols))
    history = jnp.sum(sent, axis=0)
    one_step = jnp.exp(-rate_nc)
    entering = [history]
    for k in range(1, chunks):
        entering.append(local_states[k - 1] + jnp.exp(-rate_nc * (CHUNK * k)) * history)
    entering = jnp.stack(entering) * one_step[None]
    convolved = within + jnp.sum(decay[None] * entering[:, None], axis=2)
    return convolved.reshape(local_rows, local_chan), out_weight, drive_term, own_cols


def local(post_gate, pre_gate, features, residues, rates, skip, out_weight):
    convolved, out_weight, drive_term, own_cols = recurrent_convolve(pre_gate, features, residues, rates, out_weight)
    gated_out = (post_gate.astype(jnp.float32) * (convolved + skip[None, :] * drive_term)).astype(
        jnp.bfloat16
    )
    ch_size = lax.axis_size("ch")
    ch_place = lax.axis_index("ch")
    core = lax.axis_index("pair")
    cols = out_weight.shape[1] // ch_size
    half = cols // 2

    def weight_for(offset, width, part):
        start = ((ch_place + offset) % ch_size) * cols + part * width
        return lax.dynamic_slice_in_dim(out_weight, start, width, axis=1)

    pieces = []
    for k in range(1, ch_size):
        ring = [(src, (src + k) % ch_size) for src in range(ch_size)]
        pieces.append(lax.ppermute(weight_for(k, half, core), "ch", ring))
    gated_out, *pieces = lax.optimization_barrier((gated_out, *pieces))
    fetched = jnp.stack(pieces)
    swapped = lax.ppermute(fetched, "pair", [(0, 1), (1, 0)])
    received = {}
    for k in sorted(range(1, ch_size), key=lambda k: -min(k, ch_size - k)):
        ring = [(src, (src + k) % ch_size) for src in range(ch_size)]
        received[k] = lax.ppermute(gated_out, "ch", ring)
    gated_parts = [gated_out] + [received[k] for k in range(1, ch_size)]
    remote = jnp.zeros((ch_size - 1, fetched.shape[1], cols), out_weight.dtype)
    remote = lax.dynamic_update_slice_in_dim(remote, fetched, core * half, axis=2)
    remote = lax.dynamic_update_slice_in_dim(remote, swapped, (1 - core) * half, axis=2)
    weight_rows = jnp.concatenate(
        [own_cols, remote.reshape(-1, cols)], axis=0
    )
    mixed = jnp.dot(
        jnp.concatenate(gated_parts, axis=1),
        weight_rows,
        preferred_element_type=jnp.float32,
    )
    return mixed.astype(jnp.bfloat16)


def solution(mesh):
    in_specs = (
        P(("pair", "tr"), "ch"),
        P(("pair", "tr"), "ch"),
        P(("pair", "tr"), "ch"),
        P("ch", None),
        P("ch", None),
        P("ch"),
        P("ch", None),
    )
    out_specs = P(("pair", "tr"), "ch")
    return jax.shard_map(local, mesh=mesh, in_specs=in_specs, out_specs=out_specs, check_vma=False)
```

```python
import jax
import jax.numpy as jnp
from jax import lax
from jax.sharding import PartitionSpec as P

CHUNK = 128


def sequence_place():
    return lax.axis_index("pair") * lax.axis_size("tr") + lax.axis_index("tr")


def split3(values):
    first = lax.reduce_precision(values, exponent_bits=8, mantissa_bits=7)
    rest = values - first
    second = lax.reduce_precision(rest, exponent_bits=8, mantissa_bits=7)
    third = rest - second
    return (
        first.astype(jnp.bfloat16),
        second.astype(jnp.bfloat16),
        third.astype(jnp.bfloat16),
    )


def state_of(pre_gate, features, rate_nc):
    drive_term = pre_gate.astype(jnp.float32) * features.astype(jnp.float32)
    local_rows, local_chan = drive_term.shape
    chunks = local_rows // CHUNK
    step = jnp.arange(CHUNK, dtype=jnp.float32)[:, None, None]
    rev = jnp.exp(-rate_nc[None] * (CHUNK - 1 - step))
    x = drive_term.reshape(chunks, CHUNK, 1, local_chan)
    ends = jnp.sum(x * rev[None], axis=1)
    chunk_decay = jnp.exp(-rate_nc * CHUNK)
    state = jnp.zeros_like(ends[0])
    for k in range(chunks):
        state = chunk_decay * state + ends[k]
    return ends, state


def history_payload(own_end, partner_end, rate_nc, local_rows):
    tr_size = lax.axis_size("tr")
    tr_place = lax.axis_index("tr")
    second_core = (lax.axis_index("pair") == 1).astype(jnp.float32)
    target = jnp.arange(tr_size, dtype=jnp.int32)
    lag = (target - 1 - tr_place).astype(jnp.float32)
    own_weight = jnp.where(
        lag[:, None, None] >= 0.0,
        jnp.exp(-rate_nc[None] * (local_rows * jnp.maximum(lag, 0.0))[:, None, None]),
        0.0,
    )
    partner_lag = lag + tr_size
    partner_weight = second_core * jnp.exp(
        -rate_nc[None] * (local_rows * partner_lag)[:, None, None]
    )
    return own_weight * own_end[None] + partner_weight * partner_end[None]


def recurrent_convolve(pre_gate, features, residues, rates, out_weight):
    local_rows, local_chan = pre_gate.shape
    modes = rates.shape[1]
    chunks = local_rows // CHUNK
    seq_devices = lax.axis_size("pair") * lax.axis_size("tr")
    seq_place = sequence_place()

    rate_nc = rates.T
    step = jnp.arange(CHUNK, dtype=jnp.float32)[:, None, None]
    chunk_decay = jnp.exp(-rate_nc * CHUNK)
    partner = lax.ppermute(jnp.stack([pre_gate, features]), "pair", [(0, 1), (1, 0)])
    ends, own_end = state_of(pre_gate, features, rate_nc)
    _, partner_end = state_of(partner[0], partner[1], rate_nc)
    payload = history_payload(own_end, partner_end, rate_nc, local_rows)
    payload, out_weight, ends, pre_gate, features, rates, residues = lax.optimization_barrier(
        (payload, out_weight, ends, pre_gate, features, rates, residues)
    )
    sent = lax.all_to_all(payload, "tr", 0, 0, tiled=True)
    drive_term = pre_gate.astype(jnp.float32) * features.astype(jnp.float32)
    x = drive_term.reshape(chunks, CHUNK, 1, local_chan)
    rate_nc = rates.T
    local_states = []
    state = jnp.zeros_like(ends[0])
    for k in range(chunks):
        state = chunk_decay * state + ends[k]
        local_states.append(state)

    amplitude_nc = (residues * jnp.sqrt(-jnp.expm1(-2.0 * rates))).T
    grow = jnp.exp(rate_nc[None] * step)
    decay = amplitude_nc[None] * jnp.exp(-rate_nc[None] * step)
    scaled = (x * grow[None]).reshape(chunks, CHUNK, modes * local_chan)
    parts = split3(scaled)
    lower = (step[:, 0, 0][:, None] >= step[:, 0, 0][None, :]).astype(jnp.bfloat16)
    lower3 = jnp.concatenate([lower, lower, lower], axis=1)
    stacked = jnp.concatenate(parts, axis=1)
    cums = jnp.einsum("ji,kiz->kjz", lower3, stacked, preferred_element_type=jnp.float32)
    cums = cums.reshape(chunks, CHUNK, modes, local_chan)
    within = jnp.sum(decay[None] * cums, axis=2)

    within, sent = lax.optimization_barrier((within, sent))
    history = jnp.sum(sent, axis=0)
    one_step = jnp.exp(-rate_nc)
    entering = [history]
    for k in range(1, chunks):
        entering.append(local_states[k - 1] + jnp.exp(-rate_nc * (CHUNK * k)) * history)
    entering = jnp.stack(entering) * one_step[None]
    convolved = within + jnp.sum(decay[None] * entering[:, None], axis=2)
    return convolved.reshape(local_rows, local_chan), out_weight, drive_term


def local(post_gate, pre_gate, features, residues, rates, skip, out_weight):
    convolved, out_weight, drive_term = recurrent_convolve(pre_gate, features, residues, rates, out_weight)
    gated_out = (post_gate.astype(jnp.float32) * (convolved + skip[None, :] * drive_term)).astype(
        jnp.bfloat16
    )
    ch_size = lax.axis_size("ch")
    ch_place = lax.axis_index("ch")
    core = lax.axis_index("pair")
    cols = out_weight.shape[1] // ch_size
    half = cols // 2

    def weight_for(offset, width, part):
        start = ((ch_place + offset) % ch_size) * cols + part * width
        return lax.dynamic_slice_in_dim(out_weight, start, width, axis=1)

    pieces = []
    for k in range(1, ch_size):
        ring = [(src, (src + k) % ch_size) for src in range(ch_size)]
        pieces.append(lax.ppermute(weight_for(k, half, core), "ch", ring))
    gated_out, *pieces = lax.optimization_barrier((gated_out, *pieces))
    fetched = jnp.stack(pieces)
    swapped = lax.ppermute(fetched, "pair", [(0, 1), (1, 0)])
    received = {}
    for k in sorted(range(1, ch_size), key=lambda k: -min(k, ch_size - k)):
        ring = [(src, (src + k) % ch_size) for src in range(ch_size)]
        received[k] = lax.ppermute(gated_out, "ch", ring)
    gated_parts = [gated_out] + [received[k] for k in range(1, ch_size)]
    rows = fetched.shape[1]
    every = jnp.zeros((ch_size, rows, cols), out_weight.dtype)
    every = lax.dynamic_update_slice(every, weight_for(0, cols, 0)[None], (0, 0, 0))
    every = lax.dynamic_update_slice(every, fetched, (1, 0, core * half))
    every = lax.dynamic_update_slice(every, swapped, (1, 0, (1 - core) * half))
    weight_rows = every.reshape(ch_size * rows, cols)
    mixed = jnp.dot(
        jnp.concatenate(gated_parts, axis=1),
        weight_rows,
        preferred_element_type=jnp.float32,
    )
    return mixed.astype(jnp.bfloat16)


def solution(mesh):
    in_specs = (
        P(("pair", "tr"), "ch"),
        P(("pair", "tr"), "ch"),
        P(("pair", "tr"), "ch"),
        P("ch", None),
        P("ch", None),
        P("ch"),
        P("ch", None),
    )
    out_specs = P(("pair", "tr"), "ch")
    return jax.shard_map(local, mesh=mesh, in_specs=in_specs, out_specs=out_specs, check_vma=False)
```

```python
import jax
import jax.numpy as jnp
from jax import lax
from jax.sharding import PartitionSpec as P

CHUNK = 128


def sequence_place():
    return lax.axis_index("pair") * lax.axis_size("tr") + lax.axis_index("tr")


def split3(values):
    first = lax.reduce_precision(values, exponent_bits=8, mantissa_bits=7)
    rest = values - first
    second = lax.reduce_precision(rest, exponent_bits=8, mantissa_bits=7)
    third = rest - second
    return (
        first.astype(jnp.bfloat16),
        second.astype(jnp.bfloat16),
        third.astype(jnp.bfloat16),
    )


def state_of(pre_gate, features, rate_nc):
    drive_term = pre_gate.astype(jnp.float32) * features.astype(jnp.float32)
    local_rows, local_chan = drive_term.shape
    chunks = local_rows // CHUNK
    step = jnp.arange(CHUNK, dtype=jnp.float32)[:, None, None]
    rev = jnp.exp(-rate_nc[None] * (CHUNK - 1 - step))
    x = drive_term.reshape(chunks, CHUNK, 1, local_chan)
    ends = jnp.sum(x * rev[None], axis=1)
    chunk_decay = jnp.exp(-rate_nc * CHUNK)
    state = jnp.zeros_like(ends[0])
    for k in range(chunks):
        state = chunk_decay * state + ends[k]
    return ends, state


def history_payload(own_end, partner_end, rate_nc, local_rows):
    tr_size = lax.axis_size("tr")
    tr_place = lax.axis_index("tr")
    second_core = (lax.axis_index("pair") == 1).astype(jnp.float32)
    target = jnp.arange(tr_size, dtype=jnp.int32)
    lag = (target - 1 - tr_place).astype(jnp.float32)
    own_weight = jnp.where(
        lag[:, None, None] >= 0.0,
        jnp.exp(-rate_nc[None] * (local_rows * jnp.maximum(lag, 0.0))[:, None, None]),
        0.0,
    )
    partner_lag = lag + tr_size
    partner_weight = second_core * jnp.exp(
        -rate_nc[None] * (local_rows * partner_lag)[:, None, None]
    )
    return own_weight * own_end[None] + partner_weight * partner_end[None]


def recurrent_convolve(pre_gate, features, residues, rates, out_weight):
    local_rows, local_chan = pre_gate.shape
    modes = rates.shape[1]
    chunks = local_rows // CHUNK
    seq_devices = lax.axis_size("pair") * lax.axis_size("tr")
    seq_place = sequence_place()

    rate_nc = rates.T
    step = jnp.arange(CHUNK, dtype=jnp.float32)[:, None, None]
    chunk_decay = jnp.exp(-rate_nc * CHUNK)
    partner = lax.ppermute(jnp.stack([pre_gate, features]), "pair", [(0, 1), (1, 0)])
    ends, own_end = state_of(pre_gate, features, rate_nc)
    _, partner_end = state_of(partner[0], partner[1], rate_nc)
    payload = history_payload(own_end, partner_end, rate_nc, local_rows)
    payload, out_weight, ends, pre_gate, features, rates, residues = lax.optimization_barrier(
        (payload, out_weight, ends, pre_gate, features, rates, residues)
    )
    sent = lax.all_to_all(payload, "tr", 0, 0, tiled=True)
    drive_term = pre_gate.astype(jnp.float32) * features.astype(jnp.float32)
    x = drive_term.reshape(chunks, CHUNK, 1, local_chan)
    rate_nc = rates.T
    local_states = []
    state = jnp.zeros_like(ends[0])
    for k in range(chunks):
        state = chunk_decay * state + ends[k]
        local_states.append(state)

    amplitude_nc = (residues * jnp.sqrt(-jnp.expm1(-2.0 * rates))).T
    grow = jnp.exp(rate_nc[None] * step)
    decay = amplitude_nc[None] * jnp.exp(-rate_nc[None] * step)
    scaled = (x * grow[None]).reshape(chunks, CHUNK, modes * local_chan)
    parts = split3(scaled)
    lower = (step[:, 0, 0][:, None] >= step[:, 0, 0][None, :]).astype(jnp.bfloat16)
    lower3 = jnp.concatenate([lower, lower, lower], axis=1)
    stacked = jnp.concatenate(parts, axis=1)
    cums = jnp.einsum("ji,kiz->kjz", lower3, stacked, preferred_element_type=jnp.float32)
    cums = cums.reshape(chunks, CHUNK, modes, local_chan)
    within = jnp.sum(decay[None] * cums, axis=2)

    within, sent = lax.optimization_barrier((within, sent))
    history = jnp.sum(sent, axis=0)
    one_step = jnp.exp(-rate_nc)
    entering = [history]
    for k in range(1, chunks):
        entering.append(local_states[k - 1] + jnp.exp(-rate_nc * (CHUNK * k)) * history)
    entering = jnp.stack(entering) * one_step[None]
    convolved = within + jnp.sum(decay[None] * entering[:, None], axis=2)
    return convolved.reshape(local_rows, local_chan), out_weight, drive_term


def local(post_gate, pre_gate, features, residues, rates, skip, out_weight):
    convolved, out_weight, drive_term = recurrent_convolve(pre_gate, features, residues, rates, out_weight)
    gated_out = (post_gate.astype(jnp.float32) * (convolved + skip[None, :] * drive_term)).astype(
        jnp.bfloat16
    )
    ch_size = lax.axis_size("ch")
    ch_place = lax.axis_index("ch")
    core = lax.axis_index("pair")
    cols = out_weight.shape[1] // ch_size
    half = cols // 2

    def weight_for(offset, width, part):
        start = ((ch_place + offset) % ch_size) * cols + part * width
        return lax.dynamic_slice_in_dim(out_weight, start, width, axis=1)

    pieces = []
    for k in range(1, ch_size):
        ring = [(src, (src + k) % ch_size) for src in range(ch_size)]
        pieces.append(lax.ppermute(weight_for(k, half, core), "ch", ring))
    gated_out, *pieces = lax.optimization_barrier((gated_out, *pieces))
    fetched = jnp.stack(pieces)
    swapped = lax.ppermute(fetched, "pair", [(0, 1), (1, 0)])
    received = {}
    for k in sorted(range(1, ch_size), key=lambda k: -min(k, ch_size - k)):
        ring = [(src, (src + k) % ch_size) for src in range(ch_size)]
        received[k] = lax.ppermute(gated_out, "ch", ring)
    gated_parts = [gated_out] + [received[k] for k in range(1, ch_size)]
    remote = jnp.zeros((ch_size - 1, fetched.shape[1], cols), out_weight.dtype)
    remote = lax.dynamic_update_slice_in_dim(remote, fetched, core * half, axis=2)
    remote = lax.dynamic_update_slice_in_dim(remote, swapped, (1 - core) * half, axis=2)
    if ch_size == 4:
        early = jnp.dot(
            jnp.concatenate([gated_parts[0], gated_parts[1], gated_parts[3]], axis=1),
            jnp.concatenate([weight_for(0, cols, 0), remote[0], remote[2]], axis=0),
            preferred_element_type=jnp.float32,
        )
        mixed = early + jnp.dot(gated_parts[2], remote[1], preferred_element_type=jnp.float32)
        return mixed.astype(jnp.bfloat16)
    weight_rows = jnp.concatenate(
        [weight_for(0, cols, 0), remote.reshape(-1, cols)], axis=0
    )
    mixed = jnp.dot(
        jnp.concatenate(gated_parts, axis=1),
        weight_rows,
        preferred_element_type=jnp.float32,
    )
    return mixed.astype(jnp.bfloat16)


def solution(mesh):
    in_specs = (
        P(("pair", "tr"), "ch"),
        P(("pair", "tr"), "ch"),
        P(("pair", "tr"), "ch"),
        P("ch", None),
        P("ch", None),
        P("ch"),
        P("ch", None),
    )
    out_specs = P(("pair", "tr"), "ch")
    return jax.shard_map(local, mesh=mesh, in_specs=in_specs, out_specs=out_specs, check_vma=False)
```

```python
import jax
import jax.numpy as jnp
from jax import lax
from jax.sharding import PartitionSpec as P

CHUNK = 128


def sequence_place():
    return lax.axis_index("pair") * lax.axis_size("tr") + lax.axis_index("tr")


def split3(values):
    first = lax.reduce_precision(values, exponent_bits=8, mantissa_bits=7)
    rest = values - first
    second = lax.reduce_precision(rest, exponent_bits=8, mantissa_bits=7)
    third = rest - second
    return (
        first.astype(jnp.bfloat16),
        second.astype(jnp.bfloat16),
        third.astype(jnp.bfloat16),
    )


def state_of(pre_gate, features, rate_nc):
    drive_term = pre_gate.astype(jnp.float32) * features.astype(jnp.float32)
    local_rows, local_chan = drive_term.shape
    chunks = local_rows // CHUNK
    step = jnp.arange(CHUNK, dtype=jnp.float32)[:, None, None]
    rev = jnp.exp(-rate_nc[None] * (CHUNK - 1 - step))
    x = drive_term.reshape(chunks, CHUNK, 1, local_chan)
    ends = jnp.sum(x * rev[None], axis=1)
    chunk_decay = jnp.exp(-rate_nc * CHUNK)
    state = jnp.zeros_like(ends[0])
    for k in range(chunks):
        state = chunk_decay * state + ends[k]
    return ends, state


def history_payload(own_end, partner_end, rate_nc, local_rows):
    tr_size = lax.axis_size("tr")
    tr_place = lax.axis_index("tr")
    second_core = (lax.axis_index("pair") == 1).astype(jnp.float32)
    target = jnp.arange(tr_size, dtype=jnp.int32)
    lag = (target - 1 - tr_place).astype(jnp.float32)
    own_weight = jnp.where(
        lag[:, None, None] >= 0.0,
        jnp.exp(-rate_nc[None] * (local_rows * jnp.maximum(lag, 0.0))[:, None, None]),
        0.0,
    )
    partner_lag = lag + tr_size
    partner_weight = second_core * jnp.exp(
        -rate_nc[None] * (local_rows * partner_lag)[:, None, None]
    )
    return own_weight * own_end[None] + partner_weight * partner_end[None]


def recurrent_convolve(pre_gate, features, residues, rates, out_weight):
    local_rows, local_chan = pre_gate.shape
    modes = rates.shape[1]
    chunks = local_rows // CHUNK
    seq_devices = lax.axis_size("pair") * lax.axis_size("tr")
    seq_place = sequence_place()

    rate_nc = rates.T
    step = jnp.arange(CHUNK, dtype=jnp.float32)[:, None, None]
    chunk_decay = jnp.exp(-rate_nc * CHUNK)
    partner = lax.ppermute(jnp.stack([pre_gate, features]), "pair", [(0, 1), (1, 0)])
    ends, own_end = state_of(pre_gate, features, rate_nc)
    _, partner_end = state_of(partner[0], partner[1], rate_nc)
    payload = history_payload(own_end, partner_end, rate_nc, local_rows)
    payload, out_weight, ends, pre_gate, features, rates, residues = lax.optimization_barrier(
        (payload, out_weight, ends, pre_gate, features, rates, residues)
    )
    sent = lax.all_to_all(payload, "tr", 0, 0, tiled=True)
    drive_term = pre_gate.astype(jnp.float32) * features.astype(jnp.float32)
    x = drive_term.reshape(chunks, CHUNK, 1, local_chan)
    rate_nc = rates.T
    local_states = []
    state = jnp.zeros_like(ends[0])
    for k in range(chunks):
        state = chunk_decay * state + ends[k]
        local_states.append(state)

    amplitude_nc = (residues * jnp.sqrt(-jnp.expm1(-2.0 * rates))).T
    grow = jnp.exp(rate_nc[None] * step)
    decay = amplitude_nc[None] * jnp.exp(-rate_nc[None] * step)
    scaled = (x * grow[None]).reshape(chunks, CHUNK, modes * local_chan)
    parts = split3(scaled)
    lower = (step[:, 0, 0][:, None] >= step[:, 0, 0][None, :]).astype(jnp.bfloat16)
    lower3 = jnp.concatenate([lower, lower, lower], axis=1)
    stacked = jnp.concatenate(parts, axis=1)
    cums = jnp.einsum("ji,kiz->kjz", lower3, stacked, preferred_element_type=jnp.float32)
    cums = cums.reshape(chunks, CHUNK, modes, local_chan)
    within = jnp.sum(decay[None] * cums, axis=2)

    within, sent = lax.optimization_barrier((within, sent))
    history = jnp.sum(sent, axis=0)
    one_step = jnp.exp(-rate_nc)
    entering = [history]
    for k in range(1, chunks):
        entering.append(local_states[k - 1] + jnp.exp(-rate_nc * (CHUNK * k)) * history)
    entering = jnp.stack(entering) * one_step[None]
    convolved = within + jnp.sum(decay[None] * entering[:, None], axis=2)
    return convolved.reshape(local_rows, local_chan), out_weight, drive_term


def local(post_gate, pre_gate, features, residues, rates, skip, out_weight):
    convolved, out_weight, drive_term = recurrent_convolve(pre_gate, features, residues, rates, out_weight)
    gated_out = (post_gate.astype(jnp.float32) * (convolved + skip[None, :] * drive_term)).astype(
        jnp.bfloat16
    )
    ch_size = lax.axis_size("ch")
    ch_place = lax.axis_index("ch")
    core = lax.axis_index("pair")
    cols = out_weight.shape[1] // ch_size
    half = cols // 2

    def weight_for(offset, width, part):
        start = ((ch_place + offset) % ch_size) * cols + part * width
        return lax.dynamic_slice_in_dim(out_weight, start, width, axis=1)

    pieces = []
    for k in range(1, ch_size):
        ring = [(src, (src + k) % ch_size) for src in range(ch_size)]
        pieces.append(lax.ppermute(weight_for(k, half, core), "ch", ring))
    received = {}
    for k in sorted(range(1, ch_size), key=lambda k: -min(k, ch_size - k)):
        ring = [(src, (src + k) % ch_size) for src in range(ch_size)]
        received[k] = lax.ppermute(gated_out, "ch", ring)
    order = sorted(received)
    tied = lax.optimization_barrier(tuple(received[k] for k in order) + tuple(pieces))
    received = dict(zip(order, tied[: len(order)]))
    pieces = list(tied[len(order):])
    fetched = jnp.stack(pieces)
    swapped = lax.ppermute(fetched, "pair", [(0, 1), (1, 0)])
    gated_parts = [gated_out] + [received[k] for k in range(1, ch_size)]
    remote = jnp.zeros((ch_size - 1, fetched.shape[1], cols), out_weight.dtype)
    remote = lax.dynamic_update_slice_in_dim(remote, fetched, core * half, axis=2)
    remote = lax.dynamic_update_slice_in_dim(remote, swapped, (1 - core) * half, axis=2)
    weight_rows = jnp.concatenate(
        [weight_for(0, cols, 0), remote.reshape(-1, cols)], axis=0
    )
    mixed = jnp.dot(
        jnp.concatenate(gated_parts, axis=1),
        weight_rows,
        preferred_element_type=jnp.float32,
    )
    return mixed.astype(jnp.bfloat16)


def solution(mesh):
    in_specs = (
        P(("pair", "tr"), "ch"),
        P(("pair", "tr"), "ch"),
        P(("pair", "tr"), "ch"),
        P("ch", None),
        P("ch", None),
        P("ch"),
        P("ch", None),
    )
    out_specs = P(("pair", "tr"), "ch")
    return jax.shard_map(local, mesh=mesh, in_specs=in_specs, out_specs=out_specs, check_vma=False)
```
